32 devices in a mesh: section: 2 (over x), tm: 4 (over z), space: 4 (over y, core).
Axes of the slice: x: 2, y: 2, z: 4, core: 2. Of those that a mesh axis runs over, the one named last changes fastest.
Arguments:
- video: bfloat16 [2, 8, 16, 512, 128], P('section', 'tm', 'space'), may hold values from -6 to 6
- weights: bfloat16 [2, 9, 384, 128], P('section'), may hold values from -0.109375 to 0.109375
Outputs:
- decoded: bfloat16 [2, 8, 16, 512, 128], P('section', 'tm', 'space')
The draws below stay inside these ranges and needn't reach their ends.
All inputs are finite; a program needn't handle non-finite values.
Results may differ from the reference program's by a relative error of at most 0.0095.
Values may be sent and summed in bfloat16 or wider, within the bound.
No kernel may reach another device: no remote copies, remote signals or barrier semaphores. Data moves between devices by JAX's collectives and lax.ppermute only.
A program may use at most 128 MiB of HBM per device.

```python
import jax
import jax.numpy as jnp
from jax import lax

C = 128
WID = 512
FRAMES = 8
HEIGHT = 16
MICRO = 2


def block_scale(own_key, dims, cuts, smallest, high):
    loudness, own = 1.0, jax.random.fold_in(own_key, 6)
    for axis_at, parts in cuts:
        draws = jnp.exp(jax.random.uniform(jax.random.fold_in(own, axis_at), (parts,), jnp.float32, smallest / len(cuts), high / len(cuts)))
        loudness = loudness * jnp.repeat(draws, dims[axis_at] // parts).reshape([-1 if axis == axis_at else 1 for axis in range(len(dims))])
    return loudness


def gaussian(own_key, dims, scale, reach, pieces=(), held_as=jnp.bfloat16):
    factor_of = block_scale(own_key, dims, pieces, -0.22, 0.18) if pieces else 1.0
    array = jax.random.normal(own_key, dims, jnp.float32) * scale * factor_of
    return jnp.minimum(jnp.maximum(array, -reach), reach).astype(held_as)


def setup_inputs(seed: int = 0) -> dict:
    splits = jax.random.split(jax.random.key(seed), 3)
    return {
        "video": gaussian(splits[0], (MICRO, FRAMES, HEIGHT, WID, C), 1.0, 6.0, ((0, 2), (1, 4), (2, 4))),
        "weights": gaussian(splits[1], (2, 9, 3 * C, C), (27 * C) ** -0.5, 0.109375, ((0, 2),)),
    }


def conv_block(clip, taps):
    frames, rows, width, chans = clip.shape
    act = jax.nn.silu(clip.astype(jnp.float32)).astype(jnp.bfloat16)
    padded = jnp.pad(act, ((2, 0), (1, 1), (1, 1), (0, 0)))
    joined = jnp.concatenate([padded[:, :, 0:width], padded[:, :, 1:width + 1], padded[:, :, 2:width + 2]], axis=-1)
    total = jnp.zeros((frames * rows * width, chans), jnp.float32)
    for time_tap in range(3):
        for row_tap in range(3):
            slab = joined[time_tap:time_tap + frames, row_tap:row_tap + rows]
            total = total + jnp.dot(slab.reshape(-1, 3 * chans), taps[time_tap * 3 + row_tap], preferred_element_type=jnp.float32)
    return (clip.astype(jnp.float32) + total.reshape(clip.shape)).astype(jnp.bfloat16)


def reference(video, weights):
    def both_blocks(clip):
        hidden = conv_block(clip, weights[0])
        return conv_block(hidden, weights[1])
    return lax.map(both_blocks, video)
```

```python
import jax
import jax.numpy as jnp
from jax import lax
from jax.sharding import PartitionSpec as P


def from_behind(block, axis, distance):
    devices = range(lax.axis_size(axis))
    route = [(i - distance, i) for i in devices if i - distance in devices]
    return lax.ppermute(block, axis, route)


def padded_2(cells, sides, width):
    for axis, dim in sides:
        count = lax.axis_size(axis)
        ends = count - 1
        head = lax.slice_in_dim(cells, 0, width, axis=dim)
        tail = lax.slice_in_dim(cells, cells.shape[dim] - width, cells.shape[dim], axis=dim)
        cells = jnp.concatenate(
            [
                lax.ppermute(tail, axis, [(i, (i + 1) % count) for i in range(ends)]),
                cells,
                lax.ppermute(head, axis, [((i + 1) % count, i) for i in range(ends)]),
            ],
            axis=dim,
        )
    return cells


def conv_block(clip, taps):
    frames, rows, width, chans = clip.shape
    act = jax.nn.silu(clip.astype(jnp.float32)).astype(jnp.bfloat16)
    carried = from_behind(act, "tm", 1)
    extended = jnp.concatenate([carried, act], axis=0)
    padded = padded_2(extended, (("space", 1),), 1)
    kernel = taps.reshape(3, 3, 3, chans, chans)
    total = lax.conv_general_dilated(
        padded[None],
        kernel,
        window_strides=(1, 1, 1),
        padding=((0, 0), (0, 0), (1, 1)),
        dimension_numbers=("NDHWC", "DHWIO", "NDHWC"),
        preferred_element_type=jnp.float32,
    )[0]
    return (clip.astype(jnp.float32) + total).astype(jnp.bfloat16)


def body(video, weights):
    all_taps = lax.all_gather(weights, "section", axis=0, tiled=True)
    hidden = conv_block(video[0], all_taps[0])
    finished = conv_block(hidden, all_taps[1])
    return finished[None]


def solution(mesh):
    return jax.shard_map(
        body,
        mesh=mesh,
        in_specs=(P("section", "tm", "space", None, None), P("section", None, None, None)),
        out_specs=P("section", "tm", "space", None, None),
        check_vma=False,
    )
```

```python
import jax
import jax.numpy as jnp
from jax import lax
from jax.sharding import PartitionSpec as P


def shift_tm(x):
    n = lax.axis_size("tm")
    return lax.ppermute(x, "tm", [(i, i + 1) for i in range(n - 1)])


def with_halo_rows(x):
    n = lax.axis_size("space")
    top = lax.ppermute(x[..., -1:, :, :], "space", [(i, i + 1) for i in range(n - 1)])
    bottom = lax.ppermute(x[..., :1, :, :], "space", [(i + 1, i) for i in range(n - 1)])
    return jnp.concatenate([top, x, bottom], axis=-3)


def conv_hw(frame, kern):
    return lax.conv_general_dilated(
        frame[None],
        kern,
        window_strides=(1, 1),
        padding=((0, 0), (1, 1)),
        dimension_numbers=("NHWC", "HWIO", "NHWC"),
        preferred_element_type=jnp.float32,
    )[0]


def silu(x):
    return jax.nn.silu(x.astype(jnp.float32)).astype(jnp.bfloat16)


def conv_block(clip, taps):
    frames, rows, width, chans = clip.shape
    assert frames == 2
    k = taps.reshape(3, 3, 3, chans, chans)
    act = silu(clip)
    carried_1 = shift_tm(act[1])
    own = with_halo_rows(act)
    y_own0 = conv_hw(own[0], jnp.concatenate([k[2], k[1]], axis=-1))
    part0 = y_own0[..., :chans]
    part1 = y_own0[..., chans:] + conv_hw(own[1], k[2])
    act0, carried_1 = lax.optimization_barrier((act[0], carried_1))
    carried_2 = shift_tm(act0)
    y_c1 = conv_hw(with_halo_rows(carried_1), jnp.concatenate([k[1], k[0]], axis=-1))
    out1 = (clip[1].astype(jnp.float32) + part1 + y_c1[..., chans:]).astype(jnp.bfloat16)
    y_c2 = conv_hw(with_halo_rows(carried_2), k[0])
    out0 = (clip[0].astype(jnp.float32) + part0 + y_c1[..., :chans] + y_c2).astype(jnp.bfloat16)
    return jnp.stack([out0, out1])


def both_taps(weights):
    local = weights[0]
    half = local.shape[1] // 2
    section = lax.axis_index("section")
    core = lax.axis_index("space") % 2
    n_space = lax.axis_size("space")
    mine = lax.dynamic_slice_in_dim(local, core * half, half, axis=1)
    got = lax.ppermute(mine, "section", [(0, 1), (1, 0)])
    other = lax.ppermute(got, "space", [(i, i ^ 1) for i in range(n_space)])
    low = jnp.where(core == 0, got, other)
    high = jnp.where(core == 0, other, got)
    remote = jnp.concatenate([low, high], axis=1)
    first = jnp.where(section == 0, local, remote)
    second = jnp.where(section == 0, remote, local)
    return first, second


def body(video, weights):
    first, second = both_taps(weights)
    hidden = conv_block(video[0], first)
    finished = conv_block(hidden, second)
    return finished[None]


def solution(mesh):
    return jax.shard_map(
        body,
        mesh=mesh,
        in_specs=(P("section", "tm", "space", None, None), P("section", None, None, None)),
        out_specs=P("section", "tm", "space", None, None),
        check_vma=False,
    )
```

```python
import jax
import jax.numpy as jnp
from jax import lax
from jax.sharding import PartitionSpec as P


def shift_tm(x):
    n = lax.axis_size("tm")
    return lax.ppermute(x, "tm", [(i, i + 1) for i in range(n - 1)])


def with_halo_rows(x):
    n = lax.axis_size("space")
    top = lax.ppermute(x[..., -1:, :, :], "space", [(i, i + 1) for i in range(n - 1)])
    bottom = lax.ppermute(x[..., :1, :, :], "space", [(i + 1, i) for i in range(n - 1)])
    return jnp.concatenate([top, x, bottom], axis=-3)


def silu(x):
    return jax.nn.silu(x.astype(jnp.float32)).astype(jnp.bfloat16)


def conv3(ext, kern, time_pad):
    return lax.conv_general_dilated(
        ext[None],
        kern,
        window_strides=(1, 1, 1),
        padding=(time_pad, (0, 0), (1, 1)),
        dimension_numbers=("NDHWC", "DHWIO", "NDHWC"),
        preferred_element_type=jnp.float32,
    )[0]


def conv_block(clip, taps):
    frames, rows, width, chans = clip.shape
    assert frames == 2
    k = taps.reshape(3, 3, 3, chans, chans)
    act = silu(clip)
    carried = shift_tm(act)
    own = conv3(with_halo_rows(act), k[1:], (1, 0))
    carried, own = lax.optimization_barrier((carried, own))
    far = conv3(with_halo_rows(carried), k[:2], (0, 1))
    return (clip.astype(jnp.float32) + own + far).astype(jnp.bfloat16)


def body(video, weights):
    all_taps = lax.all_gather(weights, "section", axis=0, tiled=True)
    hidden = conv_block(video[0], all_taps[0])
    finished = conv_block(hidden, all_taps[1])
    return finished[None]


def solution(mesh):
    return jax.shard_map(
        body,
        mesh=mesh,
        in_specs=(P("section", "tm", "space", None, None), P("section", None, None, None)),
        out_specs=P("section", "tm", "space", None, None),
        check_vma=False,
    )
```

```python
import jax
import jax.numpy as jnp
from jax import lax
from jax.experimental import pallas as pl
from jax.experimental.pallas import tpu as pltpu
from jax.sharding import PartitionSpec as P


def shift_tm(x):
    n = lax.axis_size("tm")
    return lax.ppermute(x, "tm", [(i, i + 1) for i in range(n - 1)])


def silu(x):
    return jax.nn.silu(x.astype(jnp.float32)).astype(jnp.bfloat16)


def conv_kernel(carried_ref, act_ref, top_ref, bottom_ref, clip_ref, w_ref, out_ref):
    frames, rows, width, chans = clip_ref.shape
    back = carried_ref.shape[0]

    def slab(f, j):
        if j == 0:
            return top_ref[f, 0]
        if j == rows + 1:
            return bottom_ref[f, 0]
        if f < back:
            return carried_ref[f, j - 1]
        return act_ref[f - back, j - 1]

    column = lax.broadcasted_iota(jnp.int32, (width, chans), 0)
    for t in range(frames):
        for h in range(rows):
            lhs = jnp.concatenate(
                [slab(t + back - 2 + a, h + r) for a in range(3) for r in range(3)], axis=-1
            )
            z = jnp.dot(lhs, w_ref[...], preferred_element_type=jnp.float32)
            left = pltpu.roll(z[:, :chans], 1, 0)
            right = pltpu.roll(z[:, 2 * chans :], width - 1, 0)
            left = jnp.where(column == 0, 0.0, left)
            right = jnp.where(column == width - 1, 0.0, right)
            total = z[:, chans : 2 * chans] + left + right
            out_ref[t, h] = (clip_ref[t, h].astype(jnp.float32) + total).astype(out_ref.dtype)


def tap_matrix(taps):
    nine, three_c, chans = taps.shape
    return (
        taps.reshape(nine, 3, chans, chans)
        .transpose(0, 2, 1, 3)
        .reshape(nine * chans, 3 * chans)
    )


def fused_conv(carried, act, top, bottom, clip, w_mat):
    frames, rows, width, chans = clip.shape
    flops = 2 * frames * rows * width * w_mat.shape[0] * w_mat.shape[1]
    nbytes = 2 * (carried.size + act.size + top.size + bottom.size + 2 * clip.size + w_mat.size)
    return pl.pallas_call(
        conv_kernel,
        out_shape=jax.ShapeDtypeStruct(clip.shape, clip.dtype),
        cost_estimate=pl.CostEstimate(flops=flops, bytes_accessed=nbytes, transcendentals=0),
    )(carried, act, top, bottom, clip, w_mat)


def conv_block(clip, w_mat):
    frames = clip.shape[0]
    assert frames == 2
    act = silu(clip)
    carried = shift_tm(act)
    n = lax.axis_size("space")
    last_rows = jnp.concatenate([carried[:, -1:], act[:, -1:]], axis=0)
    first_rows = jnp.concatenate([carried[:, :1], act[:, :1]], axis=0)
    top = lax.ppermute(last_rows, "space", [(i, i + 1) for i in range(n - 1)])
    bottom = lax.ppermute(first_rows, "space", [(i + 1, i) for i in range(n - 1)])
    return fused_conv(carried, act, top, bottom, clip, w_mat)


def body(video, weights):
    all_taps = lax.all_gather(weights, "section", axis=0, tiled=True)
    hidden = conv_block(video[0], tap_matrix(all_taps[0]))
    finished = conv_block(hidden, tap_matrix(all_taps[1]))
    return finished[None]


def solution(mesh):
    return jax.shard_map(
        body,
        mesh=mesh,
        in_specs=(P("section", "tm", "space", None, None), P("section", None, None, None)),
        out_specs=P("section", "tm", "space", None, None),
        check_vma=False,
    )
```

```python
import jax
import jax.numpy as jnp
from jax import lax
from jax.experimental import pallas as pl
from jax.experimental.pallas import tpu as pltpu
from jax.sharding import PartitionSpec as P


def shift_tm(x):
    n = lax.axis_size("tm")
    return lax.ppermute(x, "tm", [(i, i + 1) for i in range(n - 1)])


def silu(x):
    return jax.nn.silu(x.astype(jnp.float32)).astype(jnp.bfloat16)


def own_kernel(act_ref, base_ref, w_ref, out_ref):
    conv_kernel("own", None, act_ref, None, None, base_ref, w_ref, out_ref)


def rest_kernel(carried_ref, act_ref, top_ref, bottom_ref, base_ref, w_ref, out_ref):
    conv_kernel("rest", carried_ref, act_ref, top_ref, bottom_ref, base_ref, w_ref, out_ref)


def conv_kernel(part, carried_ref, act_ref, top_ref, bottom_ref, base_ref, w_ref, out_ref):
    frames, rows, width, chans = base_ref.shape
    back = act_ref.shape[0]
    group = 3 * chans

    def slab(f, j):
        if j == 0:
            return top_ref[f, 0]
        if j == rows + 1:
            return bottom_ref[f, 0]
        if f < back:
            return carried_ref[f, j - 1]
        return act_ref[f - back, j - 1]

    column = lax.broadcasted_iota(jnp.int32, (width, chans), 0)
    for t in range(frames):
        for h in range(rows):
            z = None
            for a in range(3):
                f = t + back - 2 + a
                if part == "own" and f >= back:
                    taps = [r for r in range(3) if 1 <= h + r <= rows]
                elif part == "rest" and f < back:
                    taps = [0, 1, 2]
                elif part == "rest":
                    taps = [r for r in range(3) if not 1 <= h + r <= rows]
                else:
                    taps = []
                if not taps:
                    continue
                lhs = jnp.concatenate([slab(f, h + r) for r in taps], axis=-1)
                lo = a * group + taps[0] * chans
                w = w_ref[lo : lo + len(taps) * chans, :]
                term = jnp.dot(lhs, w, preferred_element_type=jnp.float32)
                z = term if z is None else z + term
            left = pltpu.roll(z[:, :chans], 1, 0)
            right = pltpu.roll(z[:, 2 * chans :], width - 1, 0)
            left = jnp.where(column == 0, 0.0, left)
            right = jnp.where(column == width - 1, 0.0, right)
            total = z[:, chans : 2 * chans] + left + right
            out_ref[t, h] = (base_ref[t, h].astype(jnp.float32) + total).astype(out_ref.dtype)


def tap_matrix(taps):
    nine, three_c, chans = taps.shape
    return (
        taps.reshape(nine, 3, chans, chans)
        .transpose(0, 2, 1, 3)
        .reshape(nine * chans, 3 * chans)
    )


def conv_part(kernel, operands, base, w_mat, out_dtype):
    frames, rows, width, chans = base.shape
    flops = frames * rows * width * w_mat.shape[0] * w_mat.shape[1]
    nbytes = sum(x.size * x.dtype.itemsize for x in operands) + 2 * base.size * 4 + w_mat.size * 2
    return pl.pallas_call(
        kernel,
        out_shape=jax.ShapeDtypeStruct(base.shape, out_dtype),
        cost_estimate=pl.CostEstimate(flops=flops, bytes_accessed=nbytes, transcendentals=0),
    )(*operands, base, w_mat)


def conv_block(clip, w_mat):
    frames = clip.shape[0]
    assert frames == 2
    act = silu(clip)
    carried = shift_tm(act)
    partial = conv_part(own_kernel, (act,), clip, w_mat, jnp.float32)
    carried, partial = lax.optimization_barrier((carried, partial))
    n = lax.axis_size("space")
    last_rows = jnp.concatenate([carried[:, -1:], act[:, -1:]], axis=0)
    first_rows = jnp.concatenate([carried[:, :1], act[:, :1]], axis=0)
    top = lax.ppermute(last_rows, "space", [(i, i + 1) for i in range(n - 1)])
    bottom = lax.ppermute(first_rows, "space", [(i + 1, i) for i in range(n - 1)])
    return conv_part(rest_kernel, (carried, act, top, bottom), partial, w_mat, clip.dtype)


def body(video, weights):
    all_taps = lax.all_gather(weights, "section", axis=0, tiled=True)
    hidden = conv_block(video[0], tap_matrix(all_taps[0]))
    finished = conv_block(hidden, tap_matrix(all_taps[1]))
    return finished[None]


def solution(mesh):
    return jax.shard_map(
        body,
        mesh=mesh,
        in_specs=(P("section", "tm", "space", None, None), P("section", None, None, None)),
        out_specs=P("section", "tm", "space", None, None),
        check_vma=False,
    )
```

```python
import jax
import jax.numpy as jnp
from jax import lax
from jax.experimental import pallas as pl
from jax.experimental.pallas import tpu as pltpu
from jax.sharding import PartitionSpec as P


def shift_tm(x):
    n = lax.axis_size("tm")
    return lax.ppermute(x, "tm", [(i, i + 1) for i in range(n - 1)])


def silu(x):
    return jax.nn.silu(x.astype(jnp.float32)).astype(jnp.bfloat16)


def conv_kernel(carried_ref, act_ref, top_ref, bottom_ref, clip_ref, w_ref, out_ref):
    frames, rows, width, chans = clip_ref.shape
    back = carried_ref.shape[0]

    def slab(f, j):
        if j == 0:
            return top_ref[f, 0]
        if j == rows + 1:
            return bottom_ref[f, 0]
        if f < back:
            return carried_ref[f, j - 1]
        return act_ref[f - back, j - 1]

    column = lax.broadcasted_iota(jnp.int32, (width, chans), 0)
    for t in range(frames):
        for h in range(rows):
            lhs = jnp.concatenate(
                [slab(t + back - 2 + a, h + r) for a in range(3) for r in range(3)], axis=-1
            )
            z = jnp.dot(lhs, w_ref[...], preferred_element_type=jnp.float32)
            left = pltpu.roll(z[:, :chans], 1, 0)
            right = pltpu.roll(z[:, 2 * chans :], width - 1, 0)
            left = jnp.where(column == 0, 0.0, left)
            right = jnp.where(column == width - 1, 0.0, right)
            total = z[:, chans : 2 * chans] + left + right
            out_ref[t, h] = (clip_ref[t, h].astype(jnp.float32) + total).astype(out_ref.dtype)


def tap_matrix(taps):
    nine, three_c, chans = taps.shape
    return (
        taps.reshape(nine, 3, chans, chans)
        .transpose(0, 2, 1, 3)
        .reshape(nine * chans, 3 * chans)
    )


def fused_conv(carried, act, top, bottom, clip, w_mat):
    frames, rows, width, chans = clip.shape
    flops = 2 * frames * rows * width * w_mat.shape[0] * w_mat.shape[1]
    nbytes = 2 * (carried.size + act.size + top.size + bottom.size + 2 * clip.size + w_mat.size)
    return pl.pallas_call(
        conv_kernel,
        out_shape=jax.ShapeDtypeStruct(clip.shape, clip.dtype),
        cost_estimate=pl.CostEstimate(flops=flops, bytes_accessed=nbytes, transcendentals=0),
    )(carried, act, top, bottom, clip, w_mat)


def conv_block(clip, w_mat):
    frames = clip.shape[0]
    assert frames == 2
    act = silu(clip)
    carried = shift_tm(act)
    n = lax.axis_size("space")
    last_rows = jnp.concatenate([carried[:, -1:], act[:, -1:]], axis=0)
    first_rows = jnp.concatenate([carried[:, :1], act[:, :1]], axis=0)
    top = lax.ppermute(last_rows, "space", [(i, i + 1) for i in range(n - 1)])
    bottom = lax.ppermute(first_rows, "space", [(i + 1, i) for i in range(n - 1)])
    return fused_conv(carried, act, top, bottom, clip, w_mat)


def both_taps(weights):
    local = weights[0]
    half = local.shape[1] // 2
    section = lax.axis_index("section")
    core = lax.axis_index("space") % 2
    n_space = lax.axis_size("space")
    mine = lax.dynamic_slice_in_dim(local, core * half, half, axis=1)
    got = lax.ppermute(mine, "section", [(0, 1), (1, 0)])
    other = lax.ppermute(got, "space", [(i, i ^ 1) for i in range(n_space)])
    low = jnp.where(core == 0, got, other)
    high = jnp.where(core == 0, other, got)
    remote = jnp.concatenate([low, high], axis=1)
    first = jnp.where(section == 0, local, remote)
    second = jnp.where(section == 0, remote, local)
    return first, second


def body(video, weights):
    first, second = both_taps(weights)
    hidden = conv_block(video[0], tap_matrix(first))
    finished = conv_block(hidden, tap_matrix(second))
    return finished[None]


def solution(mesh):
    return jax.shard_map(
        body,
        mesh=mesh,
        in_specs=(P("section", "tm", "space", None, None), P("section", None, None, None)),
        out_specs=P("section", "tm", "space", None, None),
        check_vma=False,
    )
```

```python
import jax
import jax.numpy as jnp
from jax import lax
from jax.experimental import pallas as pl
from jax.experimental.pallas import tpu as pltpu
from jax.sharding import PartitionSpec as P


def shift_tm(x):
    n = lax.axis_size("tm")
    return lax.ppermute(x, "tm", [(i, i + 1) for i in range(n - 1)])


def silu(x):
    return jax.nn.silu(x.astype(jnp.float32)).astype(jnp.bfloat16)


def conv_kernel(carried_ref, act_ref, top_ref, bottom_ref, clip_ref, w_ref, out_ref):
    frames, rows, width, chans = clip_ref.shape
    back = carried_ref.shape[0]

    def slab(f, j):
        if j == 0:
            return top_ref[f, 0]
        if j == rows + 1:
            return bottom_ref[f, 0]
        if f < back:
            return carried_ref[f, j - 1]
        return act_ref[f - back, j - 1]

    column = lax.broadcasted_iota(jnp.int32, (width, chans), 0)
    for t in range(frames):
        for h in range(rows):
            lhs = jnp.concatenate(
                [slab(t + back - 2 + a, h + r) for a in range(3) for r in range(3)], axis=-1
            )
            z = jnp.dot(lhs, w_ref[...], preferred_element_type=jnp.float32)
            left = pltpu.roll(z[:, :chans], 1, 0)
            right = pltpu.roll(z[:, 2 * chans :], width - 1, 0)
            left = jnp.where(column == 0, 0.0, left)
            right = jnp.where(column == width - 1, 0.0, right)
            total = z[:, chans : 2 * chans] + left + right
            out_ref[t, h] = (clip_ref[t, h].astype(jnp.float32) + total).astype(out_ref.dtype)


def tap_matrix(taps):
    nine, three_c, chans = taps.shape
    return (
        taps.reshape(nine, 3, chans, chans)
        .transpose(0, 2, 1, 3)
        .reshape(nine * chans, 3 * chans)
    )


def fused_conv(carried, act, top, bottom, clip, w_mat):
    frames, rows, width, chans = clip.shape
    flops = 2 * frames * rows * width * w_mat.shape[0] * w_mat.shape[1]
    nbytes = 2 * (carried.size + act.size + top.size + bottom.size + 2 * clip.size + w_mat.size)
    return pl.pallas_call(
        conv_kernel,
        out_shape=jax.ShapeDtypeStruct(clip.shape, clip.dtype),
        cost_estimate=pl.CostEstimate(flops=flops, bytes_accessed=nbytes, transcendentals=0),
    )(carried, act, top, bottom, clip, w_mat)


def conv_block(clip, w_mat, ahead=()):
    frames = clip.shape[0]
    assert frames == 2
    act = silu(clip)
    carried = shift_tm(act)
    carried, w_mat, ahead = lax.optimization_barrier((carried, w_mat, ahead))
    n = lax.axis_size("space")
    last_rows = jnp.concatenate([carried[:, -1:], act[:, -1:]], axis=0)
    first_rows = jnp.concatenate([carried[:, :1], act[:, :1]], axis=0)
    top = lax.ppermute(last_rows, "space", [(i, i + 1) for i in range(n - 1)])
    bottom = lax.ppermute(first_rows, "space", [(i + 1, i) for i in range(n - 1)])
    return fused_conv(carried, act, top, bottom, clip, w_mat), ahead


def both_taps(weights):
    local = weights[0]
    half = local.shape[1] // 2
    section = lax.axis_index("section")
    core = lax.axis_index("space") % 2
    n_space = lax.axis_size("space")
    mine = lax.dynamic_slice_in_dim(local, core * half, half, axis=1)
    got = lax.ppermute(mine, "section", [(0, 1), (1, 0)])
    other = lax.ppermute(got, "space", [(i, i ^ 1) for i in range(n_space)])
    low = jnp.where(core == 0, got, other)
    high = jnp.where(core == 0, other, got)
    remote = jnp.concatenate([low, high], axis=1)
    first = jnp.where(section == 0, local, remote)
    second = jnp.where(section == 0, remote, local)
    return first, second


def body(video, weights):
    first, second = both_taps(weights)
    hidden, second_mat = conv_block(video[0], tap_matrix(first), tap_matrix(second))
    finished, _ = conv_block(hidden, second_mat)
    return finished[None]


def solution(mesh):
    return jax.shard_map(
        body,
        mesh=mesh,
        in_specs=(P("section", "tm", "space", None, None), P("section", None, None, None)),
        out_specs=P("section", "tm", "space", None, None),
        check_vma=False,
    )
```

```python
import jax
import jax.numpy as jnp
from jax import lax
from jax.experimental import pallas as pl
from jax.experimental.pallas import tpu as pltpu
from jax.sharding import PartitionSpec as P


def shift_tm(x):
    n = lax.axis_size("tm")
    return lax.ppermute(x, "tm", [(i, i + 1) for i in range(n - 1)])


def silu(x):
    return jax.nn.silu(x.astype(jnp.float32)).astype(jnp.bfloat16)


def conv_kernel(carried_ref, act_ref, top_ref, bottom_ref, clip_ref, w_ref, out_ref):
    frames, rows, width, chans = clip_ref.shape
    back = carried_ref.shape[0]

    def slab(f, j):
        if j == 0:
            return top_ref[f, 0]
        if j == rows + 1:
            return bottom_ref[f, 0]
        if f < back:
            return carried_ref[f, j - 1]
        return act_ref[f - back, j - 1]

    column = lax.broadcasted_iota(jnp.int32, (width, chans), 0)
    for t in range(frames):
        for h in range(rows):
            lhs = jnp.concatenate(
                [slab(t + back - 2 + a, h + r) for a in range(3) for r in range(3)], axis=-1
            )
            z = jnp.dot(lhs, w_ref[...], preferred_element_type=jnp.float32)
            left = pltpu.roll(z[:, :chans], 1, 0)
            right = pltpu.roll(z[:, 2 * chans :], width - 1, 0)
            left = jnp.where(column == 0, 0.0, left)
            right = jnp.where(column == width - 1, 0.0, right)
            total = z[:, chans : 2 * chans] + left + right
            out_ref[t, h] = (clip_ref[t, h].astype(jnp.float32) + total).astype(out_ref.dtype)


def tap_matrix(taps):
    nine, three_c, chans = taps.shape
    return (
        taps.reshape(nine, 3, chans, chans)
        .transpose(0, 2, 1, 3)
        .reshape(nine * chans, 3 * chans)
    )


def fused_conv(carried, act, top, bottom, clip, w_mat):
    frames, rows, width, chans = clip.shape
    flops = 2 * frames * rows * width * w_mat.shape[0] * w_mat.shape[1]
    nbytes = 2 * (carried.size + act.size + top.size + bottom.size + 2 * clip.size + w_mat.size)
    return pl.pallas_call(
        conv_kernel,
        out_shape=jax.ShapeDtypeStruct(clip.shape, clip.dtype),
        cost_estimate=pl.CostEstimate(flops=flops, bytes_accessed=nbytes, transcendentals=0),
    )(carried, act, top, bottom, clip, w_mat)


def conv_block(clip, w_mat, tie_taps):
    frames = clip.shape[0]
    assert frames == 2
    act = silu(clip)
    carried = shift_tm(act)
    if tie_taps:
        carried, w_mat = lax.optimization_barrier((carried, w_mat))
    n = lax.axis_size("space")
    last_rows = jnp.concatenate([carried[:, -1:], act[:, -1:]], axis=0)
    first_rows = jnp.concatenate([carried[:, :1], act[:, :1]], axis=0)
    top = lax.ppermute(last_rows, "space", [(i, i + 1) for i in range(n - 1)])
    bottom = lax.ppermute(first_rows, "space", [(i + 1, i) for i in range(n - 1)])
    return fused_conv(carried, act, top, bottom, clip, w_mat)


def both_taps(weights):
    local = weights[0]
    half = local.shape[1] // 2
    section = lax.axis_index("section")
    core = lax.axis_index("space") % 2
    n_space = lax.axis_size("space")
    mine = lax.dynamic_slice_in_dim(local, core * half, half, axis=1)
    got = lax.ppermute(mine, "section", [(0, 1), (1, 0)])
    other = lax.ppermute(got, "space", [(i, i ^ 1) for i in range(n_space)])
    low = jnp.where(core == 0, got, other)
    high = jnp.where(core == 0, other, got)
    remote = jnp.concatenate([low, high], axis=1)
    first = jnp.where(section == 0, local, remote)
    second = jnp.where(section == 0, remote, local)
    return first, second


def body(video, weights):
    first, second = both_taps(weights)
    hidden = conv_block(video[0], tap_matrix(first), False)
    finished = conv_block(hidden, tap_matrix(second), True)
    return finished[None]


def solution(mesh):
    return jax.shard_map(
        body,
        mesh=mesh,
        in_specs=(P("section", "tm", "space", None, None), P("section", None, None, None)),
        out_specs=P("section", "tm", "space", None, None),
        check_vma=False,
    )
```

```python
import functools

import jax
import jax.numpy as jnp
from jax import lax
from jax.experimental import pallas as pl
from jax.experimental.pallas import tpu as pltpu
from jax.sharding import PartitionSpec as P


def shift_tm(x):
    n = lax.axis_size("tm")
    return lax.ppermute(x, "tm", [(i, i + 1) for i in range(n - 1)])


def silu(x):
    return jax.nn.silu(x.astype(jnp.float32)).astype(jnp.bfloat16)


def frame_kernel(t, n_out, *refs):
    if t == 1:
        c1_ref, a0_ref, a1_ref, top_a, bot_a, base_ref, w_ref = refs[:7]
        sources = [(c1_ref, top_a, bot_a, 0), (a0_ref, top_a, bot_a, 1), (a1_ref, top_a, bot_a, 2)]
    else:
        c2_ref, c1_ref, a0_ref, top_a, bot_a, top_b, bot_b, base_ref, w_ref = refs[:9]
        sources = [(c2_ref, top_b, bot_b, 0), (c1_ref, top_a, bot_a, 0), (a0_ref, top_a, bot_a, 1)]
    outs = refs[len(refs) - n_out :]
    rows, width, chans = base_ref.shape

    def slab(a, j):
        ref, top, bottom, halo = sources[a]
        if j == 0:
            return top[halo, 0]
        if j == rows + 1:
            return bottom[halo, 0]
        return ref[j - 1]

    column = lax.broadcasted_iota(jnp.int32, (width, chans), 0)
    for h in range(rows):
        lhs = jnp.concatenate([slab(a, h + r) for a in range(3) for r in range(3)], axis=-1)
        z = jnp.dot(lhs, w_ref[...], preferred_element_type=jnp.float32)
        left = pltpu.roll(z[:, :chans], 1, 0)
        right = pltpu.roll(z[:, 2 * chans :], width - 1, 0)
        left = jnp.where(column == 0, 0.0, left)
        right = jnp.where(column == width - 1, 0.0, right)
        total = z[:, chans : 2 * chans] + left + right
        out = (base_ref[h].astype(jnp.float32) + total).astype(outs[0].dtype)
        outs[0][h] = out
        if len(outs) == 2:
            wide = out.astype(jnp.float32)
            outs[1][h] = (wide / (1.0 + jnp.exp(-wide))).astype(outs[1].dtype)


def tap_matrix(taps):
    nine, three_c, chans = taps.shape
    return (
        taps.reshape(nine, 3, chans, chans)
        .transpose(0, 2, 1, 3)
        .reshape(nine * chans, 3 * chans)
    )


def frame_conv(t, operands, base, w_mat, with_act):
    rows, width, chans = base.shape
    flops = 2 * rows * width * w_mat.shape[0] * w_mat.shape[1]
    nbytes = sum(x.size * x.dtype.itemsize for x in operands) + 3 * base.size * 2 + w_mat.size * 2
    shape = jax.ShapeDtypeStruct(base.shape, base.dtype)
    return pl.pallas_call(
        functools.partial(frame_kernel, t, 2 if with_act else 1),
        out_shape=(shape, shape) if with_act else (shape,),
        cost_estimate=pl.CostEstimate(flops=flops, bytes_accessed=nbytes, transcendentals=0),
    )(*operands, base, w_mat)


def conv_block(frames_in, acts, w_mat, with_act):
    x0, x1 = frames_in
    a0, a1 = acts
    n = lax.axis_size("space")
    down = [(i, i + 1) for i in range(n - 1)]
    up = [(i + 1, i) for i in range(n - 1)]
    c1 = shift_tm(a1)
    a0, c1 = lax.optimization_barrier((a0, c1))
    c2 = shift_tm(a0)
    top_a = lax.ppermute(jnp.stack([c1[-1:], a0[-1:], a1[-1:]]), "space", down)
    bot_a = lax.ppermute(jnp.stack([c1[:1], a0[:1], a1[:1]]), "space", up)
    outs1 = frame_conv(1, (c1, a0, a1, top_a, bot_a), x1, w_mat, with_act)
    top_b = lax.ppermute(c2[None, -1:], "space", down)
    bot_b = lax.ppermute(c2[None, :1], "space", up)
    outs0 = frame_conv(0, (c2, c1, a0, top_a, bot_a, top_b, bot_b), x0, w_mat, with_act)
    return outs0, outs1


def both_taps(weights):
    local = weights[0]
    half = local.shape[1] // 2
    section = lax.axis_index("section")
    core = lax.axis_index("space") % 2
    n_space = lax.axis_size("space")
    mine = lax.dynamic_slice_in_dim(local, core * half, half, axis=1)
    got = lax.ppermute(mine, "section", [(0, 1), (1, 0)])
    other = lax.ppermute(got, "space", [(i, i ^ 1) for i in range(n_space)])
    low = jnp.where(core == 0, got, other)
    high = jnp.where(core == 0, other, got)
    remote = jnp.concatenate([low, high], axis=1)
    first = jnp.where(section == 0, local, remote)
    second = jnp.where(section == 0, remote, local)
    return first, second


def body(video, weights):
    first, second = both_taps(weights)
    clip = video[0]
    assert clip.shape[0] == 2
    x0, x1 = clip[0], clip[1]
    a1 = silu(x1)
    a0 = silu(x0)
    (h0, s0), (h1, s1) = conv_block((x0, x1), (a0, a1), tap_matrix(first), True)
    (o0,), (o1,) = conv_block((h0, h1), (s0, s1), tap_matrix(second), False)
    return jnp.stack([o0, o1])[None]


def solution(mesh):
    return jax.shard_map(
        body,
        mesh=mesh,
        in_specs=(P("section", "tm", "space", None, None), P("section", None, None, None)),
        out_specs=P("section", "tm", "space", None, None),
        check_vma=False,
    )
```

```python
import functools

import jax
import jax.numpy as jnp
from jax import lax
from jax.experimental import pallas as pl
from jax.experimental.pallas import tpu as pltpu
from jax.sharding import PartitionSpec as P


def shift_tm(x):
    n = lax.axis_size("tm")
    return lax.ppermute(x, "tm", [(i, i + 1) for i in range(n - 1)])


def silu(x):
    return jax.nn.silu(x.astype(jnp.float32)).astype(jnp.bfloat16)


def frame_kernel(t, n_out, merge, *refs):
    if t == 1:
        c1_ref, a0_ref, a1_ref, top_a, bot_a = refs[:5]
        sources = [(c1_ref, top_a, bot_a, 0), (a0_ref, top_a, bot_a, 1), (a1_ref, top_a, bot_a, 2)]
        at = 5
    else:
        c2_ref, c1_ref, a0_ref, top_a, bot_a, top_b, bot_b = refs[:7]
        sources = [(c2_ref, top_b, bot_b, 0), (c1_ref, top_a, bot_a, 0), (a0_ref, top_a, bot_a, 1)]
        at = 7
    if merge:
        other_ref = refs[at]
        at += 1
    base_ref, w_ref = refs[at], refs[at + 1]
    outs = refs[len(refs) - n_out :]
    rows, width, chans = base_ref.shape

    def slab(a, j):
        ref, top, bottom, halo = sources[a]
        if j == 0:
            return top[halo, 0]
        if j == rows + 1:
            return bottom[halo, 0]
        return ref[j - 1]

    column = lax.broadcasted_iota(jnp.int32, (width, chans), 0)
    for h in range(rows):
        lhs = jnp.concatenate([slab(a, h + r) for a in range(3) for r in range(3)], axis=-1)
        z = jnp.dot(lhs, w_ref[...], preferred_element_type=jnp.float32)
        left = pltpu.roll(z[:, :chans], 1, 0)
        right = pltpu.roll(z[:, 2 * chans :], width - 1, 0)
        left = jnp.where(column == 0, 0.0, left)
        right = jnp.where(column == width - 1, 0.0, right)
        total = z[:, chans : 2 * chans] + left + right
        out = (base_ref[h].astype(jnp.float32) + total).astype(outs[0].dtype)
        if merge:
            outs[0][t, h] = out
        else:
            outs[0][h] = out
        if len(outs) == 2:
            wide = out.astype(jnp.float32)
            outs[1][h] = (wide / (1.0 + jnp.exp(-wide))).astype(outs[1].dtype)
    if merge:
        outs[0][1 - t] = other_ref[...]


def tap_matrix(taps):
    nine, three_c, chans = taps.shape
    return (
        taps.reshape(nine, 3, chans, chans)
        .transpose(0, 2, 1, 3)
        .reshape(nine * chans, 3 * chans)
    )


def frame_conv(t, operands, base, w_mat, with_act, merge=None):
    rows, width, chans = base.shape
    if merge is not None:
        operands = operands + (merge,)
    flops = 2 * rows * width * w_mat.shape[0] * w_mat.shape[1]
    nbytes = sum(x.size * x.dtype.itemsize for x in operands) + 3 * base.size * 2 + w_mat.size * 2
    shape = jax.ShapeDtypeStruct(base.shape, base.dtype)
    if merge is not None:
        shape = jax.ShapeDtypeStruct((2,) + base.shape, base.dtype)
    return pl.pallas_call(
        functools.partial(frame_kernel, t, 2 if with_act else 1, merge is not None),
        out_shape=(shape, shape) if with_act else (shape,),
        cost_estimate=pl.CostEstimate(flops=flops, bytes_accessed=nbytes, transcendentals=0),
    )(*operands, base, w_mat)


def conv_block(frames_in, acts, w_mat, with_act, merge):
    x0, x1 = frames_in
    a0, a1 = acts
    n = lax.axis_size("space")
    down = [(i, i + 1) for i in range(n - 1)]
    up = [(i + 1, i) for i in range(n - 1)]
    c1 = shift_tm(a1)
    a0, c1 = lax.optimization_barrier((a0, c1))
    c2 = shift_tm(a0)
    top_a = lax.ppermute(jnp.stack([c1[-1:], a0[-1:], a1[-1:]]), "space", down)
    bot_a = lax.ppermute(jnp.stack([c1[:1], a0[:1], a1[:1]]), "space", up)
    outs1 = frame_conv(1, (c1, a0, a1, top_a, bot_a), x1, w_mat, with_act)
    top_b = lax.ppermute(c2[None, -1:], "space", down)
    bot_b = lax.ppermute(c2[None, :1], "space", up)
    last = outs1[0] if merge else None
    outs0 = frame_conv(0, (c2, c1, a0, top_a, bot_a, top_b, bot_b), x0, w_mat, with_act, last)
    return outs0, outs1


def both_taps(weights):
    local = tap_matrix(weights[0])
    half = local.shape[0] // 2
    section = lax.axis_index("section")
    core = lax.axis_index("space") % 2
    n_space = lax.axis_size("space")
    mine = lax.dynamic_slice_in_dim(local, core * half, half, axis=0)
    got = lax.ppermute(mine, "section", [(0, 1), (1, 0)])
    other = lax.ppermute(got, "space", [(i, i ^ 1) for i in range(n_space)])
    low = jnp.where(core == 0, got, other)
    high = jnp.where(core == 0, other, got)
    remote = jnp.concatenate([low, high], axis=0)
    first = jnp.where(section == 0, local, remote)
    second = jnp.where(section == 0, remote, local)
    return first, second


def body(video, weights):
    first, second = both_taps(weights)
    clip = video[0]
    assert clip.shape[0] == 2
    x0, x1 = clip[0], clip[1]
    a1 = silu(x1)
    a0 = silu(x0)
    (h0, s0), (h1, s1) = conv_block((x0, x1), (a0, a1), first, True, False)
    (whole,), _ = conv_block((h0, h1), (s0, s1), second, False, True)
    return whole[None]


def solution(mesh):
    return jax.shard_map(
        body,
        mesh=mesh,
        in_specs=(P("section", "tm", "space", None, None), P("section", None, None, None)),
        out_specs=P("section", "tm", "space", None, None),
        check_vma=False,
    )
```

```python
import functools

import jax
import jax.numpy as jnp
from jax import lax
from jax.experimental import pallas as pl
from jax.experimental.pallas import tpu as pltpu
from jax.sharding import PartitionSpec as P


def shift_tm(x):
    n = lax.axis_size("tm")
    return lax.ppermute(x, "tm", [(i, i + 1) for i in range(n - 1)])


def silu(x):
    return jax.nn.silu(x.astype(jnp.float32)).astype(jnp.bfloat16)


def frame_kernel(t, n_out, merge, *refs):
    if t == 1:
        c1_ref, a0_ref, a1_ref, top_a, bot_a = refs[:5]
        sources = [(c1_ref, top_a, bot_a, 0), (a0_ref, top_a, bot_a, 1), (a1_ref, top_a, bot_a, 2)]
        at = 5
    else:
        c2_ref, c1_ref, a0_ref, top_a, bot_a, top_b, bot_b = refs[:7]
        sources = [(c2_ref, top_b, bot_b, 0), (c1_ref, top_a, bot_a, 0), (a0_ref, top_a, bot_a, 1)]
        at = 7
    if merge:
        other_ref = refs[at]
        at += 1
    base_ref, w_ref = refs[at], refs[at + 1]
    outs = refs[len(refs) - n_out :]
    rows, width, chans = base_ref.shape

    def slab(a, j):
        ref, top, bottom, halo = sources[a]
        if j == 0:
            return top[halo, 0]
        if j == rows + 1:
            return bottom[halo, 0]
        return ref[j - 1]

    column = lax.broadcasted_iota(jnp.int32, (width, chans), 0)
    for h in range(rows):
        lhs = jnp.concatenate([slab(a, h + r) for a in range(3) for r in range(3)], axis=-1)
        z = jnp.dot(lhs, w_ref[...], preferred_element_type=jnp.float32)
        left = pltpu.roll(z[:, :chans], 1, 0)
        right = pltpu.roll(z[:, 2 * chans :], width - 1, 0)
        left = jnp.where(column == 0, 0.0, left)
        right = jnp.where(column == width - 1, 0.0, right)
        total = z[:, chans : 2 * chans] + left + right
        out = (base_ref[h].astype(jnp.float32) + total).astype(outs[0].dtype)
        if merge:
            outs[0][t, h] = out
        else:
            outs[0][h] = out
        if len(outs) == 2:
            wide = out.astype(jnp.float32)
            outs[1][h] = (wide / (1.0 + jnp.exp(-wide))).astype(outs[1].dtype)
    if merge:
        outs[0][1 - t] = other_ref[...]


def tap_matrix(taps):
    nine, three_c, chans = taps.shape
    return (
        taps.reshape(nine, 3, chans, chans)
        .transpose(0, 2, 1, 3)
        .reshape(nine * chans, 3 * chans)
    )


def frame_conv(t, operands, base, w_mat, with_act, merge=None):
    rows, width, chans = base.shape
    if merge is not None:
        operands = operands + (merge,)
    flops = 2 * rows * width * w_mat.shape[0] * w_mat.shape[1]
    nbytes = sum(x.size * x.dtype.itemsize for x in operands) + 3 * base.size * 2 + w_mat.size * 2
    shape = jax.ShapeDtypeStruct(base.shape, base.dtype)
    if merge is not None:
        shape = jax.ShapeDtypeStruct((2,) + base.shape, base.dtype)
    return pl.pallas_call(
        functools.partial(frame_kernel, t, 2 if with_act else 1, merge is not None),
        out_shape=(shape, shape) if with_act else (shape,),
        cost_estimate=pl.CostEstimate(flops=flops, bytes_accessed=nbytes, transcendentals=0),
    )(*operands, base, w_mat)


def conv_block(frames_in, acts, w_mat, with_act, merge):
    x0, x1 = frames_in
    a0, a1 = acts
    n = lax.axis_size("space")
    down = [(i, i + 1) for i in range(n - 1)]
    up = [(i + 1, i) for i in range(n - 1)]
    c1 = shift_tm(a1)
    if merge:
        c1, w_mat = lax.optimization_barrier((c1, w_mat))
        w_mat = pick_second(*w_mat)
    a0, c1 = lax.optimization_barrier((a0, c1))
    c2 = shift_tm(a0)
    top_a = lax.ppermute(jnp.stack([c1[-1:], a0[-1:], a1[-1:]]), "space", down)
    bot_a = lax.ppermute(jnp.stack([c1[:1], a0[:1], a1[:1]]), "space", up)
    outs1 = frame_conv(1, (c1, a0, a1, top_a, bot_a), x1, w_mat, with_act)
    top_b = lax.ppermute(c2[None, -1:], "space", down)
    bot_b = lax.ppermute(c2[None, :1], "space", up)
    last = outs1[0] if merge else None
    outs0 = frame_conv(0, (c2, c1, a0, top_a, bot_a, top_b, bot_b), x0, w_mat, with_act, last)
    return outs0, outs1


def both_taps(weights):
    local = tap_matrix(weights[0])
    half = local.shape[0] // 2
    section = lax.axis_index("section")
    core = lax.axis_index("space") % 2
    n_space = lax.axis_size("space")
    mine = lax.dynamic_slice_in_dim(local, core * half, half, axis=0)
    got = lax.ppermute(mine, "section", [(0, 1), (1, 0)])
    other = lax.ppermute(got, "space", [(i, i ^ 1) for i in range(n_space)])
    low = jnp.where(core == 0, got, other)
    high = jnp.where(core == 0, other, got)
    remote = jnp.concatenate([low, high], axis=0)
    first = jnp.where(section == 0, local, remote)
    return first, (local, remote)


def pick_second(local, remote):
    return jnp.where(lax.axis_index("section") == 0, remote, local)


def body(video, weights):
    first, second = both_taps(weights)
    clip = video[0]
    assert clip.shape[0] == 2
    x0, x1 = clip[0], clip[1]
    a1 = silu(x1)
    a0 = silu(x0)
    (h0, s0), (h1, s1) = conv_block((x0, x1), (a0, a1), first, True, False)
    (whole,), _ = conv_block((h0, h1), (s0, s1), second, False, True)
    return whole[None]


def solution(mesh):
    return jax.shard_map(
        body,
        mesh=mesh,
        in_specs=(P("section", "tm", "space", None, None), P("section", None, None, None)),
        out_specs=P("section", "tm", "space", None, None),
        check_vma=False,
    )
```

```python
import functools

import jax
import jax.numpy as jnp
from jax import lax
from jax.experimental import pallas as pl
from jax.experimental.pallas import tpu as pltpu
from jax.sharding import PartitionSpec as P


def shift_tm(x):
    n = lax.axis_size("tm")
    return lax.ppermute(x, "tm", [(i, i + 1) for i in range(n - 1)])


def silu(x):
    return jax.nn.silu(x.astype(jnp.float32)).astype(jnp.bfloat16)


def frame_kernel(t, n_out, merge, *refs):
    if t == 1:
        c1_ref, a0_ref, a1_ref, top_a, bot_a = refs[:5]
        sources = [(c1_ref, top_a, bot_a, 0), (a0_ref, top_a, bot_a, 1), (a1_ref, top_a, bot_a, 2)]
        at = 5
    else:
        c2_ref, c1_ref, a0_ref, top_a, bot_a, top_b, bot_b = refs[:7]
        sources = [(c2_ref, top_b, bot_b, 0), (c1_ref, top_a, bot_a, 0), (a0_ref, top_a, bot_a, 1)]
        at = 7
    if merge:
        other_ref = refs[at]
        at += 1
    base_ref, w_ref = refs[at], refs[at + 1]
    outs = refs[len(refs) - n_out :]
    rows, width, chans = base_ref.shape

    def slab(a, j):
        ref, top, bottom, halo = sources[a]
        if j == 0:
            return top[halo, 0]
        if j == rows + 1:
            return bottom[halo, 0]
        return ref[j - 1]

    column = lax.broadcasted_iota(jnp.int32, (width, chans), 0)
    for h in range(rows):
        lhs = jnp.concatenate([slab(a, h + r) for a in range(3) for r in range(3)], axis=-1)
        z = jnp.dot(lhs, w_ref[...], preferred_element_type=jnp.float32)
        left = pltpu.roll(z[:, :chans], 1, 0)
        right = pltpu.roll(z[:, 2 * chans :], width - 1, 0)
        left = jnp.where(column == 0, 0.0, left)
        right = jnp.where(column == width - 1, 0.0, right)
        total = z[:, chans : 2 * chans] + left + right
        out = (base_ref[h].astype(jnp.float32) + total).astype(outs[0].dtype)
        if merge:
            outs[0][t, h] = out
        else:
            outs[0][h] = out
        if len(outs) == 2:
            wide = out.astype(jnp.float32)
            outs[1][h] = (wide / (1.0 + jnp.exp(-wide))).astype(outs[1].dtype)
    if merge:
        outs[0][1 - t] = other_ref[...]


def tap_matrix(taps):
    nine, three_c, chans = taps.shape
    return (
        taps.reshape(nine, 3, chans, chans)
        .transpose(0, 2, 1, 3)
        .reshape(nine * chans, 3 * chans)
    )


def frame_conv(t, operands, base, w_mat, with_act, merge=None):
    rows, width, chans = base.shape
    if merge is not None:
        operands = operands + (merge,)
    flops = 2 * rows * width * w_mat.shape[0] * w_mat.shape[1]
    nbytes = sum(x.size * x.dtype.itemsize for x in operands) + 3 * base.size * 2 + w_mat.size * 2
    shape = jax.ShapeDtypeStruct(base.shape, base.dtype)
    if merge is not None:
        shape = jax.ShapeDtypeStruct((2,) + base.shape, base.dtype)
    return pl.pallas_call(
        functools.partial(frame_kernel, t, 2 if with_act else 1, merge is not None),
        out_shape=(shape, shape) if with_act else (shape,),
        cost_estimate=pl.CostEstimate(flops=flops, bytes_accessed=nbytes, transcendentals=0),
    )(*operands, base, w_mat)


def conv_block(frames_in, acts, w_mat, with_act, merge):
    x0, x1 = frames_in
    a0, a1 = acts
    n = lax.axis_size("space")
    down = [(i, i + 1) for i in range(n - 1)]
    up = [(i + 1, i) for i in range(n - 1)]
    c1 = shift_tm(a1)
    a0, c1 = lax.optimization_barrier((a0, c1))
    c2 = shift_tm(a0)
    top_a = lax.ppermute(jnp.stack([c1[-1:], a0[-1:], a1[-1:]]), "space", down)
    bot_a = lax.ppermute(jnp.stack([c1[:1], a0[:1], a1[:1]]), "space", up)
    outs1 = frame_conv(1, (c1, a0, a1, top_a, bot_a), x1, w_mat, with_act)
    c2, outs1 = lax.optimization_barrier((c2, outs1))
    top_b = lax.ppermute(c2[None, -1:], "space", down)
    bot_b = lax.ppermute(c2[None, :1], "space", up)
    last = outs1[0] if merge else None
    outs0 = frame_conv(0, (c2, c1, a0, top_a, bot_a, top_b, bot_b), x0, w_mat, with_act, last)
    return outs0, outs1


def both_taps(weights):
    local = tap_matrix(weights[0])
    half = local.shape[0] // 2
    section = lax.axis_index("section")
    core = lax.axis_index("space") % 2
    n_space = lax.axis_size("space")
    mine = lax.dynamic_slice_in_dim(local, core * half, half, axis=0)
    got = lax.ppermute(mine, "section", [(0, 1), (1, 0)])
    other = lax.ppermute(got, "space", [(i, i ^ 1) for i in range(n_space)])
    low = jnp.where(core == 0, got, other)
    high = jnp.where(core == 0, other, got)
    remote = jnp.concatenate([low, high], axis=0)
    first = jnp.where(section == 0, local, remote)
    second = jnp.where(section == 0, remote, local)
    return first, second


def body(video, weights):
    first, second = both_taps(weights)
    clip = video[0]
    assert clip.shape[0] == 2
    x0, x1 = clip[0], clip[1]
    a1 = silu(x1)
    a0 = silu(x0)
    (h0, s0), (h1, s1) = conv_block((x0, x1), (a0, a1), first, True, False)
    (whole,), _ = conv_block((h0, h1), (s0, s1), second, False, True)
    return whole[None]


def solution(mesh):
    return jax.shard_map(
        body,
        mesh=mesh,
        in_specs=(P("section", "tm", "space", None, None), P("section", None, None, None)),
        out_specs=P("section", "tm", "space", None, None),
        check_vma=False,
    )
```

```python
import functools

import jax
import jax.numpy as jnp
from jax import lax
from jax.experimental import pallas as pl
from jax.experimental.pallas import tpu as pltpu
from jax.sharding import PartitionSpec as P


def shift_tm(x):
    n = lax.axis_size("tm")
    return lax.ppermute(x, "tm", [(i, i + 1) for i in range(n - 1)])


def silu(x):
    return jax.nn.silu(x.astype(jnp.float32)).astype(jnp.bfloat16)


def frame_kernel(t, n_out, merge, *refs):
    if t == 1:
        c1_ref, a0_ref, a1_ref, top_a, bot_a = refs[:5]
        sources = [(c1_ref, top_a, bot_a, 0), (a0_ref, top_a, bot_a, 1), (a1_ref, top_a, bot_a, 2)]
        at = 5
    else:
        c2_ref, c1_ref, a0_ref, top_a, bot_a, top_b, bot_b = refs[:7]
        sources = [(c2_ref, top_b, bot_b, 0), (c1_ref, top_a, bot_a, 0), (a0_ref, top_a, bot_a, 1)]
        at = 7
    if merge:
        other_ref = refs[at]
        at += 1
    base_ref, w_ref = refs[at], refs[at + 1]
    outs = refs[len(refs) - n_out :]
    rows, width, chans = base_ref.shape

    def slab(a, j):
        ref, top, bottom, halo = sources[a]
        if j == 0:
            return top[halo, 0]
        if j == rows + 1:
            return bottom[halo, 0]
        return ref[j - 1]

    column = lax.broadcasted_iota(jnp.int32, (width, chans), 0)
    for h in range(rows):
        lhs = jnp.concatenate([slab(a, h + r) for a in range(3) for r in range(3)], axis=-1)
        z = jnp.dot(lhs, w_ref[...], preferred_element_type=jnp.float32)
        left = pltpu.roll(z[:, :chans], 1, 0)
        right = pltpu.roll(z[:, 2 * chans :], width - 1, 0)
        left = jnp.where(column == 0, 0.0, left)
        right = jnp.where(column == width - 1, 0.0, right)
        total = z[:, chans : 2 * chans] + left + right
        out = (base_ref[h].astype(jnp.float32) + total).astype(outs[0].dtype)
        if merge:
            outs[0][t, h] = out
        else:
            outs[0][h] = out
        if len(outs) == 2:
            wide = out.astype(jnp.float32)
            outs[1][h] = (wide / (1.0 + jnp.exp(-wide))).astype(outs[1].dtype)
    if merge:
        outs[0][1 - t] = other_ref[...]


def tap_matrix(taps):
    nine, three_c, chans = taps.shape
    return (
        taps.reshape(nine, 3, chans, chans)
        .transpose(0, 2, 1, 3)
        .reshape(nine * chans, 3 * chans)
    )


def frame_conv(t, operands, base, w_mat, with_act, merge=None):
    rows, width, chans = base.shape
    if merge is not None:
        operands = operands + (merge,)
    flops = 2 * rows * width * w_mat.shape[0] * w_mat.shape[1]
    nbytes = sum(x.size * x.dtype.itemsize for x in operands) + 3 * base.size * 2 + w_mat.size * 2
    shape = jax.ShapeDtypeStruct(base.shape, base.dtype)
    if merge is not None:
        shape = jax.ShapeDtypeStruct((2,) + base.shape, base.dtype)
    return pl.pallas_call(
        functools.partial(frame_kernel, t, 2 if with_act else 1, merge is not None),
        out_shape=(shape, shape) if with_act else (shape,),
        cost_estimate=pl.CostEstimate(flops=flops, bytes_accessed=nbytes, transcendentals=0),
    )(*operands, base, w_mat)


def conv_block(frames_in, acts, w_mat, with_act, merge, taps=None):
    x0, x1 = frames_in
    a0, a1 = acts
    n = lax.axis_size("space")
    down = [(i, i + 1) for i in range(n - 1)]
    up = [(i + 1, i) for i in range(n - 1)]
    c1 = shift_tm(a1)
    a0, c1 = lax.optimization_barrier((a0, c1))
    c2 = shift_tm(a0)
    later = None
    if taps is not None:
        c2, got = lax.optimization_barrier((c2, taps[1]))
        w_mat, later = both_taps(taps[0], got)
    top_a = lax.ppermute(jnp.stack([c1[-1:], a0[-1:], a1[-1:]]), "space", down)
    bot_a = lax.ppermute(jnp.stack([c1[:1], a0[:1], a1[:1]]), "space", up)
    outs1 = frame_conv(1, (c1, a0, a1, top_a, bot_a), x1, w_mat, with_act)
    top_b = lax.ppermute(c2[None, -1:], "space", down)
    bot_b = lax.ppermute(c2[None, :1], "space", up)
    last = outs1[0] if merge else None
    outs0 = frame_conv(0, (c2, c1, a0, top_a, bot_a, top_b, bot_b), x0, w_mat, with_act, last)
    return outs0, outs1, later


def send_taps(weights):
    local = tap_matrix(weights[0])
    half = local.shape[0] // 2
    core = lax.axis_index("space") % 2
    mine = lax.dynamic_slice_in_dim(local, core * half, half, axis=0)
    return local, lax.ppermute(mine, "section", [(0, 1), (1, 0)])


def both_taps(local, got):
    section = lax.axis_index("section")
    core = lax.axis_index("space") % 2
    n_space = lax.axis_size("space")
    other = lax.ppermute(got, "space", [(i, i ^ 1) for i in range(n_space)])
    low = jnp.where(core == 0, got, other)
    high = jnp.where(core == 0, other, got)
    remote = jnp.concatenate([low, high], axis=0)
    first = jnp.where(section == 0, local, remote)
    second = jnp.where(section == 0, remote, local)
    return first, second


def body(video, weights):
    taps = send_taps(weights)
    clip = video[0]
    assert clip.shape[0] == 2
    x0, x1 = clip[0], clip[1]
    a1 = silu(x1)
    a0 = silu(x0)
    (h0, s0), (h1, s1), second = conv_block((x0, x1), (a0, a1), None, True, False, taps)
    (whole,), _, _ = conv_block((h0, h1), (s0, s1), second, False, True)
    return whole[None]


def solution(mesh):
    return jax.shard_map(
        body,
        mesh=mesh,
        in_specs=(P("section", "tm", "space", None, None), P("section", None, None, None)),
        out_specs=P("section", "tm", "space", None, None),
        check_vma=False,
    )
```

```python
import functools

import jax
import jax.numpy as jnp
from jax import lax
from jax.experimental import pallas as pl
from jax.experimental.pallas import tpu as pltpu
from jax.sharding import PartitionSpec as P


def shift_tm(x):
    n = lax.axis_size("tm")
    return lax.ppermute(x, "tm", [(i, i + 1) for i in range(n - 1)])


def silu(x):
    return jax.nn.silu(x.astype(jnp.float32)).astype(jnp.bfloat16)


def conv_rows(sources, base_ref, w_ref, store):
    rows, width, chans = base_ref.shape

    def slab(a, j):
        ref, top, bottom, halo = sources[a]
        if j == 0:
            return top[halo, 0]
        if j == rows + 1:
            return bottom[halo, 0]
        return ref[j - 1]

    column = lax.broadcasted_iota(jnp.int32, (width, chans), 0)
    for h in range(rows):
        lhs = jnp.concatenate([slab(a, h + r) for a in range(3) for r in range(3)], axis=-1)
        z = jnp.dot(lhs, w_ref[...], preferred_element_type=jnp.float32)
        left = pltpu.roll(z[:, :chans], 1, 0)
        right = pltpu.roll(z[:, 2 * chans :], width - 1, 0)
        left = jnp.where(column == 0, 0.0, left)
        right = jnp.where(column == width - 1, 0.0, right)
        total = z[:, chans : 2 * chans] + left + right
        store(h, base_ref[h].astype(jnp.float32) + total)


def frame_sources(t, c2_ref, c1_ref, a0_ref, a1_ref, top_a, bot_a, top_b, bot_b):
    if t == 1:
        return [(c1_ref, top_a, bot_a, 0), (a0_ref, top_a, bot_a, 1), (a1_ref, top_a, bot_a, 2)]
    return [(c2_ref, top_b, bot_b, 0), (c1_ref, top_a, bot_a, 0), (a0_ref, top_a, bot_a, 1)]


def frame_kernel(t, with_act, *refs):
    if t == 1:
        c1_ref, a0_ref, a1_ref, top_a, bot_a, base_ref, w_ref = refs[:7]
        sources = frame_sources(1, None, c1_ref, a0_ref, a1_ref, top_a, bot_a, None, None)
    else:
        c2_ref, c1_ref, a0_ref, top_a, bot_a, top_b, bot_b, base_ref, w_ref = refs[:9]
        sources = frame_sources(0, c2_ref, c1_ref, a0_ref, None, top_a, bot_a, top_b, bot_b)
    outs = refs[len(refs) - (2 if with_act else 1) :]

    def store(h, value):
        out = value.astype(outs[0].dtype)
        outs[0][h] = out
        if with_act:
            wide = out.astype(jnp.float32)
            outs[1][h] = (wide / (1.0 + jnp.exp(-wide))).astype(outs[1].dtype)

    conv_rows(sources, base_ref, w_ref, store)


def pair_kernel(c2_ref, c1_ref, a0_ref, a1_ref, top_a, bot_a, top_b, bot_b, x0_ref, x1_ref, w_ref, out_ref):
    for t, base_ref in ((1, x1_ref), (0, x0_ref)):
        sources = frame_sources(t, c2_ref, c1_ref, a0_ref, a1_ref, top_a, bot_a, top_b, bot_b)

        def store(h, value, t=t):
            out_ref[t, h] = value.astype(out_ref.dtype)

        conv_rows(sources, base_ref, w_ref, store)


def tap_matrix(taps):
    nine, three_c, chans = taps.shape
    return (
        taps.reshape(nine, 3, chans, chans)
        .transpose(0, 2, 1, 3)
        .reshape(nine * chans, 3 * chans)
    )


def frame_conv(t, operands, base, w_mat, with_act):
    rows, width, chans = base.shape
    flops = 2 * rows * width * w_mat.shape[0] * w_mat.shape[1]
    nbytes = sum(x.size * x.dtype.itemsize for x in operands) + 3 * base.size * 2 + w_mat.size * 2
    shape = jax.ShapeDtypeStruct(base.shape, base.dtype)
    return pl.pallas_call(
        functools.partial(frame_kernel, t, with_act),
        out_shape=(shape, shape) if with_act else (shape,),
        cost_estimate=pl.CostEstimate(flops=flops, bytes_accessed=nbytes, transcendentals=0),
    )(*operands, base, w_mat)


def pair_conv(operands, x0, x1, w_mat):
    rows, width, chans = x0.shape
    flops = 4 * rows * width * w_mat.shape[0] * w_mat.shape[1]
    nbytes = sum(x.size * x.dtype.itemsize for x in operands) + 4 * x0.size * 2 + w_mat.size * 2
    return pl.pallas_call(
        pair_kernel,
        out_shape=jax.ShapeDtypeStruct((2,) + x0.shape, x0.dtype),
        cost_estimate=pl.CostEstimate(flops=flops, bytes_accessed=nbytes, transcendentals=0),
    )(*operands, x0, x1, w_mat)


def conv_block(frames_in, acts, w_mat, with_act, merge):
    x0, x1 = frames_in
    a0, a1 = acts
    n = lax.axis_size("space")
    down = [(i, i + 1) for i in range(n - 1)]
    up = [(i + 1, i) for i in range(n - 1)]
    c1 = shift_tm(a1)
    a0, c1 = lax.optimization_barrier((a0, c1))
    c2 = shift_tm(a0)
    top_a = lax.ppermute(jnp.stack([c1[-1:], a0[-1:], a1[-1:]]), "space", down)
    bot_a = lax.ppermute(jnp.stack([c1[:1], a0[:1], a1[:1]]), "space", up)
    if merge:
        top_b = lax.ppermute(c2[None, -1:], "space", down)
        bot_b = lax.ppermute(c2[None, :1], "space", up)
        return pair_conv((c2, c1, a0, a1, top_a, bot_a, top_b, bot_b), x0, x1, w_mat)
    outs1 = frame_conv(1, (c1, a0, a1, top_a, bot_a), x1, w_mat, with_act)
    top_b = lax.ppermute(c2[None, -1:], "space", down)
    bot_b = lax.ppermute(c2[None, :1], "space", up)
    outs0 = frame_conv(0, (c2, c1, a0, top_a, bot_a, top_b, bot_b), x0, w_mat, with_act)
    return outs0, outs1


def both_taps(weights):
    local = tap_matrix(weights[0])
    half = local.shape[0] // 2
    section = lax.axis_index("section")
    core = lax.axis_index("space") % 2
    n_space = lax.axis_size("space")
    mine = lax.dynamic_slice_in_dim(local, core * half, half, axis=0)
    got = lax.ppermute(mine, "section", [(0, 1), (1, 0)])
    other = lax.ppermute(got, "space", [(i, i ^ 1) for i in range(n_space)])
    low = jnp.where(core == 0, got, other)
    high = jnp.where(core == 0, other, got)
    remote = jnp.concatenate([low, high], axis=0)
    first = jnp.where(section == 0, local, remote)
    second = jnp.where(section == 0, remote, local)
    return first, second


def body(video, weights):
    first, second = both_taps(weights)
    clip = video[0]
    assert clip.shape[0] == 2
    x0, x1 = clip[0], clip[1]
    a1 = silu(x1)
    a0 = silu(x0)
    (h0, s0), (h1, s1) = conv_block((x0, x1), (a0, a1), first, True, False)
    whole = conv_block((h0, h1), (s0, s1), second, False, True)
    return whole[None]


def solution(mesh):
    return jax.shard_map(
        body,
        mesh=mesh,
        in_specs=(P("section", "tm", "space", None, None), P("section", None, None, None)),
        out_specs=P("section", "tm", "space", None, None),
        check_vma=False,
    )
```

```python
import functools

import jax
import jax.numpy as jnp
from jax import lax
from jax.experimental import pallas as pl
from jax.experimental.pallas import tpu as pltpu
from jax.sharding import PartitionSpec as P


def shift_tm(x):
    n = lax.axis_size("tm")
    return lax.ppermute(x, "tm", [(i, i + 1) for i in range(n - 1)])


def silu(x):
    return jax.nn.silu(x.astype(jnp.float32)).astype(jnp.bfloat16)


def conv_rows(sources, base_ref, w_ref, store):
    rows, width, chans = base_ref.shape

    def slab(a, j):
        ref, top, bottom, halo = sources[a]
        if j == 0:
            return top[halo, 0]
        if j == rows + 1:
            return bottom[halo, 0]
        return ref[j - 1]

    column = lax.broadcasted_iota(jnp.int32, (width, chans), 0)
    for h in range(rows):
        lhs = jnp.concatenate([slab(a, h + r) for a in range(3) for r in range(3)], axis=-1)
        z = jnp.dot(lhs, w_ref[...], preferred_element_type=jnp.float32)
        left = pltpu.roll(z[:, :chans], 1, 0)
        right = pltpu.roll(z[:, 2 * chans :], width - 1, 0)
        left = jnp.where(column == 0, 0.0, left)
        right = jnp.where(column == width - 1, 0.0, right)
        total = z[:, chans : 2 * chans] + left + right
        store(h, base_ref[h].astype(jnp.float32) + total)


def frame_sources(t, c2_ref, c1_ref, a0_ref, a1_ref, top_a, bot_a, top_b, bot_b):
    if t == 1:
        return [(c1_ref, top_a, bot_a, 0), (a0_ref, top_a, bot_a, 1), (a1_ref, top_a, bot_a, 2)]
    return [(c2_ref, top_b, bot_b, 0), (c1_ref, top_a, bot_a, 0), (a0_ref, top_a, bot_a, 1)]


def frame_kernel(t, with_act, *refs):
    if t == 1:
        c1_ref, a0_ref, a1_ref, top_a, bot_a, base_ref, w_ref = refs[:7]
        sources = frame_sources(1, None, c1_ref, a0_ref, a1_ref, top_a, bot_a, None, None)
    else:
        c2_ref, c1_ref, a0_ref, top_a, bot_a, top_b, bot_b, base_ref, w_ref = refs[:9]
        sources = frame_sources(0, c2_ref, c1_ref, a0_ref, None, top_a, bot_a, top_b, bot_b)
    outs = refs[len(refs) - (2 if with_act else 1) :]

    def store(h, value):
        out = value.astype(outs[0].dtype)
        outs[0][h] = out
        if with_act:
            wide = out.astype(jnp.float32)
            outs[1][h] = (wide / (1.0 + jnp.exp(-wide))).astype(outs[1].dtype)

    conv_rows(sources, base_ref, w_ref, store)


def pair_kernel(c2_ref, c1_ref, a0_ref, a1_ref, top, bottom, x0_ref, x1_ref, w_ref, out_ref):
    frames = [c2_ref, c1_ref, a0_ref, a1_ref]
    for t, base_ref in ((1, x1_ref), (0, x0_ref)):
        sources = [(frames[t + a], top, bottom, t + a) for a in range(3)]

        def store(h, value, t=t):
            out_ref[t, h] = value.astype(out_ref.dtype)

        conv_rows(sources, base_ref, w_ref, store)


def tap_matrix(taps):
    nine, three_c, chans = taps.shape
    return (
        taps.reshape(nine, 3, chans, chans)
        .transpose(0, 2, 1, 3)
        .reshape(nine * chans, 3 * chans)
    )


def frame_conv(t, operands, base, w_mat, with_act):
    rows, width, chans = base.shape
    flops = 2 * rows * width * w_mat.shape[0] * w_mat.shape[1]
    nbytes = sum(x.size * x.dtype.itemsize for x in operands) + 3 * base.size * 2 + w_mat.size * 2
    shape = jax.ShapeDtypeStruct(base.shape, base.dtype)
    return pl.pallas_call(
        functools.partial(frame_kernel, t, with_act),
        out_shape=(shape, shape) if with_act else (shape,),
        cost_estimate=pl.CostEstimate(flops=flops, bytes_accessed=nbytes, transcendentals=0),
    )(*operands, base, w_mat)


def pair_conv(operands, x0, x1, w_mat):
    rows, width, chans = x0.shape
    flops = 4 * rows * width * w_mat.shape[0] * w_mat.shape[1]
    nbytes = sum(x.size * x.dtype.itemsize for x in operands) + 4 * x0.size * 2 + w_mat.size * 2
    return pl.pallas_call(
        pair_kernel,
        out_shape=jax.ShapeDtypeStruct((2,) + x0.shape, x0.dtype),
        cost_estimate=pl.CostEstimate(flops=flops, bytes_accessed=nbytes, transcendentals=0),
    )(*operands, x0, x1, w_mat)


def conv_block(frames_in, acts, w_mat, with_act, merge):
    x0, x1 = frames_in
    a0, a1 = acts
    n = lax.axis_size("space")
    down = [(i, i + 1) for i in range(n - 1)]
    up = [(i + 1, i) for i in range(n - 1)]
    c1 = shift_tm(a1)
    a0, c1 = lax.optimization_barrier((a0, c1))
    c2 = shift_tm(a0)
    if merge:
        top = lax.ppermute(jnp.stack([c2[-1:], c1[-1:], a0[-1:], a1[-1:]]), "space", down)
        bottom = lax.ppermute(jnp.stack([c2[:1], c1[:1], a0[:1], a1[:1]]), "space", up)
        return pair_conv((c2, c1, a0, a1, top, bottom), x0, x1, w_mat)
    top_a = lax.ppermute(jnp.stack([c1[-1:], a0[-1:], a1[-1:]]), "space", down)
    bot_a = lax.ppermute(jnp.stack([c1[:1], a0[:1], a1[:1]]), "space", up)
    outs1 = frame_conv(1, (c1, a0, a1, top_a, bot_a), x1, w_mat, with_act)
    top_b = lax.ppermute(c2[None, -1:], "space", down)
    bot_b = lax.ppermute(c2[None, :1], "space", up)
    outs0 = frame_conv(0, (c2, c1, a0, top_a, bot_a, top_b, bot_b), x0, w_mat, with_act)
    return outs0, outs1


def both_taps(weights):
    local = tap_matrix(weights[0])
    half = local.shape[0] // 2
    section = lax.axis_index("section")
    core = lax.axis_index("space") % 2
    n_space = lax.axis_size("space")
    mine = lax.dynamic_slice_in_dim(local, core * half, half, axis=0)
    got = lax.ppermute(mine, "section", [(0, 1), (1, 0)])
    other = lax.ppermute(got, "space", [(i, i ^ 1) for i in range(n_space)])
    low = jnp.where(core == 0, got, other)
    high = jnp.where(core == 0, other, got)
    remote = jnp.concatenate([low, high], axis=0)
    first = jnp.where(section == 0, local, remote)
    second = jnp.where(section == 0, remote, local)
    return first, second


def body(video, weights):
    first, second = both_taps(weights)
    clip = video[0]
    assert clip.shape[0] == 2
    x0, x1 = clip[0], clip[1]
    a1 = silu(x1)
    a0 = silu(x0)
    (h0, s0), (h1, s1) = conv_block((x0, x1), (a0, a1), first, True, False)
    whole = conv_block((h0, h1), (s0, s1), second, False, True)
    return whole[None]


def solution(mesh):
    return jax.shard_map(
        body,
        mesh=mesh,
        in_specs=(P("section", "tm", "space", None, None), P("section", None, None, None)),
        out_specs=P("section", "tm", "space", None, None),
        check_vma=False,
    )
```

```python
import functools

import jax
import jax.numpy as jnp
from jax import lax
from jax.experimental import pallas as pl
from jax.experimental.pallas import tpu as pltpu
from jax.sharding import PartitionSpec as P


def shift_tm(x):
    n = lax.axis_size("tm")
    return lax.ppermute(x, "tm", [(i, i + 1) for i in range(n - 1)])


def silu(x):
    return jax.nn.silu(x.astype(jnp.float32)).astype(jnp.bfloat16)


def conv_rows(sources, base_ref, w_ref, store):
    rows, width, chans = base_ref.shape

    def slab(a, j):
        ref, top, bottom, halo = sources[a]
        if j == 0:
            return top[halo, 0]
        if j == rows + 1:
            return bottom[halo, 0]
        return ref[j - 1]

    column = lax.broadcasted_iota(jnp.int32, (width, chans), 0)
    for h in range(rows):
        lhs = jnp.concatenate([slab(a, h + r) for a in range(3) for r in range(3)], axis=-1)
        z = jnp.dot(lhs, w_ref[...], preferred_element_type=jnp.float32)
        left = pltpu.roll(z[:, :chans], 1, 0)
        right = pltpu.roll(z[:, 2 * chans :], width - 1, 0)
        left = jnp.where(column == 0, 0.0, left)
        right = jnp.where(column == width - 1, 0.0, right)
        total = z[:, chans : 2 * chans] + left + right
        store(h, base_ref[h].astype(jnp.float32) + total)


def frame_sources(t, c2_ref, c1_ref, a0_ref, a1_ref, top_a, bot_a, top_b, bot_b):
    if t == 1:
        return [(c1_ref, top_a, bot_a, 0), (a0_ref, top_a, bot_a, 1), (a1_ref, top_a, bot_a, 2)]
    return [(c2_ref, top_b, bot_b, 0), (c1_ref, top_a, bot_a, 0), (a0_ref, top_a, bot_a, 1)]


def frame_kernel(t, with_act, *refs):
    if t == 1:
        c1_ref, a0_ref, a1_ref, top_a, bot_a, base_ref, w_ref = refs[:7]
        sources = frame_sources(1, None, c1_ref, a0_ref, a1_ref, top_a, bot_a, None, None)
    else:
        c2_ref, c1_ref, a0_ref, top_a, bot_a, top_b, bot_b, base_ref, w_ref = refs[:9]
        sources = frame_sources(0, c2_ref, c1_ref, a0_ref, None, top_a, bot_a, top_b, bot_b)
    outs = refs[len(refs) - (2 if with_act else 1) :]

    def store(h, value):
        out = value.astype(outs[0].dtype)
        outs[0][h] = out
        if with_act:
            wide = out.astype(jnp.float32)
            outs[1][h] = (wide / (1.0 + jnp.exp(-wide))).astype(outs[1].dtype)

    conv_rows(sources, base_ref, w_ref, store)


def pair_kernel(c2_ref, c1_ref, a0_ref, a1_ref, top_a, bot_a, top_b, bot_b, x0_ref, x1_ref, w_ref, out_ref):
    for t, base_ref in ((1, x1_ref), (0, x0_ref)):
        sources = frame_sources(t, c2_ref, c1_ref, a0_ref, a1_ref, top_a, bot_a, top_b, bot_b)

        def store(h, value, t=t):
            out_ref[t, h] = value.astype(out_ref.dtype)

        conv_rows(sources, base_ref, w_ref, store)


def tap_matrix(taps):
    nine, three_c, chans = taps.shape
    return (
        taps.reshape(nine, 3, chans, chans)
        .transpose(0, 2, 1, 3)
        .reshape(nine * chans, 3 * chans)
    )


def frame_conv(t, operands, base, w_mat, with_act):
    rows, width, chans = base.shape
    flops = 2 * rows * width * w_mat.shape[0] * w_mat.shape[1]
    nbytes = sum(x.size * x.dtype.itemsize for x in operands) + 3 * base.size * 2 + w_mat.size * 2
    shape = jax.ShapeDtypeStruct(base.shape, base.dtype)
    return pl.pallas_call(
        functools.partial(frame_kernel, t, with_act),
        out_shape=(shape, shape) if with_act else (shape,),
        cost_estimate=pl.CostEstimate(flops=flops, bytes_accessed=nbytes, transcendentals=0),
    )(*operands, base, w_mat)


def pair_conv(operands, x0, x1, w_mat):
    rows, width, chans = x0.shape
    flops = 4 * rows * width * w_mat.shape[0] * w_mat.shape[1]
    nbytes = sum(x.size * x.dtype.itemsize for x in operands) + 4 * x0.size * 2 + w_mat.size * 2
    return pl.pallas_call(
        pair_kernel,
        out_shape=jax.ShapeDtypeStruct((2,) + x0.shape, x0.dtype),
        cost_estimate=pl.CostEstimate(flops=flops, bytes_accessed=nbytes, transcendentals=0),
    )(*operands, x0, x1, w_mat)


def conv_block(frames_in, acts, w_mat, with_act, merge):
    x0, x1 = frames_in
    a0, a1 = acts
    n = lax.axis_size("space")
    down = [(i, i + 1) for i in range(n - 1)]
    up = [(i + 1, i) for i in range(n - 1)]
    if merge:
        c1 = shift_tm(a1)
    else:
        c1 = silu(shift_tm(x1))
    a0, c1 = lax.optimization_barrier((a0, c1))
    c2 = shift_tm(a0)
    top_a = lax.ppermute(jnp.stack([c1[-1:], a0[-1:], a1[-1:]]), "space", down)
    bot_a = lax.ppermute(jnp.stack([c1[:1], a0[:1], a1[:1]]), "space", up)
    if merge:
        top_b = lax.ppermute(c2[None, -1:], "space", down)
        bot_b = lax.ppermute(c2[None, :1], "space", up)
        return pair_conv((c2, c1, a0, a1, top_a, bot_a, top_b, bot_b), x0, x1, w_mat)
    outs1 = frame_conv(1, (c1, a0, a1, top_a, bot_a), x1, w_mat, with_act)
    top_b = lax.ppermute(c2[None, -1:], "space", down)
    bot_b = lax.ppermute(c2[None, :1], "space", up)
    outs0 = frame_conv(0, (c2, c1, a0, top_a, bot_a, top_b, bot_b), x0, w_mat, with_act)
    return outs0, outs1


def both_taps(weights):
    local = tap_matrix(weights[0])
    half = local.shape[0] // 2
    section = lax.axis_index("section")
    core = lax.axis_index("space") % 2
    n_space = lax.axis_size("space")
    mine = lax.dynamic_slice_in_dim(local, core * half, half, axis=0)
    got = lax.ppermute(mine, "section", [(0, 1), (1, 0)])
    other = lax.ppermute(got, "space", [(i, i ^ 1) for i in range(n_space)])
    low = jnp.where(core == 0, got, other)
    high = jnp.where(core == 0, other, got)
    remote = jnp.concatenate([low, high], axis=0)
    first = jnp.where(section == 0, local, remote)
    second = jnp.where(section == 0, remote, local)
    return first, second


def body(video, weights):
    first, second = both_taps(weights)
    clip = video[0]
    assert clip.shape[0] == 2
    x0, x1 = clip[0], clip[1]
    a1 = silu(x1)
    a0 = silu(x0)
    (h0, s0), (h1, s1) = conv_block((x0, x1), (a0, a1), first, True, False)
    whole = conv_block((h0, h1), (s0, s1), second, False, True)
    return whole[None]


def solution(mesh):
    return jax.shard_map(
        body,
        mesh=mesh,
        in_specs=(P("section", "tm", "space", None, None), P("section", None, None, None)),
        out_specs=P("section", "tm", "space", None, None),
        check_vma=False,
    )
```

```python
import functools

import jax
import jax.numpy as jnp
from jax import lax
from jax.experimental import pallas as pl
from jax.experimental.pallas import tpu as pltpu
from jax.sharding import PartitionSpec as P


def shift_tm(x):
    n = lax.axis_size("tm")
    return lax.ppermute(x, "tm", [(i, i + 1) for i in range(n - 1)])


def silu(x):
    return jax.nn.silu(x.astype(jnp.float32)).astype(jnp.bfloat16)


def conv_rows(sources, base_ref, w_ref, store):
    rows, width, chans = base_ref.shape

    def slab(a, j):
        ref, top, bottom, halo = sources[a]
        if j == 0:
            return top[halo, 0]
        if j == rows + 1:
            return bottom[halo, 0]
        return ref[j - 1]

    column = lax.broadcasted_iota(jnp.int32, (width, chans), 0)
    for h in range(rows):
        lhs = jnp.concatenate([slab(a, h + r) for a in range(3) for r in range(3)], axis=-1)
        z = jnp.dot(lhs, w_ref[...], preferred_element_type=jnp.float32)
        left = pltpu.roll(z[:, :chans], 1, 0)
        right = pltpu.roll(z[:, 2 * chans :], width - 1, 0)
        left = jnp.where(column == 0, 0.0, left)
        right = jnp.where(column == width - 1, 0.0, right)
        total = z[:, chans : 2 * chans] + left + right
        store(h, base_ref[h].astype(jnp.float32) + total)


def frame_sources(t, c2_ref, c1_ref, a0_ref, a1_ref, top_a, bot_a, top_b, bot_b):
    if t == 1:
        return [(c1_ref, top_a, bot_a, 0), (a0_ref, top_a, bot_a, 1), (a1_ref, top_a, bot_a, 2)]
    return [(c2_ref, top_b, bot_b, 0), (c1_ref, top_a, bot_a, 0), (a0_ref, top_a, bot_a, 1)]


def assemble(first, local_ref, got_ref, other_ref, buf):
    section = lax.axis_index("section")
    core = lax.axis_index("space") % 2
    half = got_ref.shape[0]
    use_local = section == 0 if first else section != 0

    @pl.when(use_local)
    def _():
        buf[...] = local_ref[...]

    @pl.when(jnp.logical_and(jnp.logical_not(use_local), core == 0))
    def _():
        buf[:half] = got_ref[...]
        buf[half:] = other_ref[...]

    @pl.when(jnp.logical_and(jnp.logical_not(use_local), core != 0))
    def _():
        buf[:half] = other_ref[...]
        buf[half:] = got_ref[...]

    return buf


def frame_kernel(t, with_act, first, *refs):
    buf = refs[-1]
    refs = refs[:-1]
    if t == 1:
        c1_ref, a0_ref, a1_ref, top_a, bot_a, base_ref = refs[:6]
        w_ref = assemble(first, *refs[6:9], buf)
        sources = frame_sources(1, None, c1_ref, a0_ref, a1_ref, top_a, bot_a, None, None)
    else:
        c2_ref, c1_ref, a0_ref, top_a, bot_a, top_b, bot_b, base_ref = refs[:8]
        w_ref = assemble(first, *refs[8:11], buf)
        sources = frame_sources(0, c2_ref, c1_ref, a0_ref, None, top_a, bot_a, top_b, bot_b)
    outs = refs[len(refs) - (2 if with_act else 1) :]

    def store(h, value):
        out = value.astype(outs[0].dtype)
        outs[0][h] = out
        if with_act:
            wide = out.astype(jnp.float32)
            outs[1][h] = (wide / (1.0 + jnp.exp(-wide))).astype(outs[1].dtype)

    conv_rows(sources, base_ref, w_ref, store)


def pair_kernel(first, c2_ref, c1_ref, a0_ref, a1_ref, top_a, bot_a, top_b, bot_b, x0_ref, x1_ref, local_ref, got_ref, other_ref, out_ref, buf):
    w_ref = assemble(first, local_ref, got_ref, other_ref, buf)
    for t, base_ref in ((1, x1_ref), (0, x0_ref)):
        sources = frame_sources(t, c2_ref, c1_ref, a0_ref, a1_ref, top_a, bot_a, top_b, bot_b)

        def store(h, value, t=t):
            out_ref[t, h] = value.astype(out_ref.dtype)

        conv_rows(sources, base_ref, w_ref, store)


def tap_matrix(taps):
    nine, three_c, chans = taps.shape
    return (
        taps.reshape(nine, 3, chans, chans)
        .transpose(0, 2, 1, 3)
        .reshape(nine * chans, 3 * chans)
    )


def frame_conv(t, operands, base, w_parts, with_act):
    rows, width, chans = base.shape
    first, local, got, other = w_parts
    flops = 2 * rows * width * local.shape[0] * local.shape[1]
    nbytes = sum(x.size * x.dtype.itemsize for x in operands) + 3 * base.size * 2 + local.size * 4
    shape = jax.ShapeDtypeStruct(base.shape, base.dtype)
    return pl.pallas_call(
        functools.partial(frame_kernel, t, with_act, first),
        out_shape=(shape, shape) if with_act else (shape,),
        scratch_shapes=[pltpu.VMEM(local.shape, local.dtype)],
        cost_estimate=pl.CostEstimate(flops=flops, bytes_accessed=nbytes, transcendentals=0),
    )(*operands, base, local, got, other)


def pair_conv(operands, x0, x1, w_parts):
    rows, width, chans = x0.shape
    first, local, got, other = w_parts
    flops = 4 * rows * width * local.shape[0] * local.shape[1]
    nbytes = sum(x.size * x.dtype.itemsize for x in operands) + 4 * x0.size * 2 + local.size * 4
    return pl.pallas_call(
        functools.partial(pair_kernel, first),
        out_shape=jax.ShapeDtypeStruct((2,) + x0.shape, x0.dtype),
        scratch_shapes=[pltpu.VMEM(local.shape, local.dtype)],
        cost_estimate=pl.CostEstimate(flops=flops, bytes_accessed=nbytes, transcendentals=0),
    )(*operands, x0, x1, local, got, other)


def conv_block(frames_in, acts, w_mat, with_act, merge):
    x0, x1 = frames_in
    a0, a1 = acts
    n = lax.axis_size("space")
    down = [(i, i + 1) for i in range(n - 1)]
    up = [(i + 1, i) for i in range(n - 1)]
    c1 = shift_tm(a1)
    a0, c1 = lax.optimization_barrier((a0, c1))
    c2 = shift_tm(a0)
    top_a = lax.ppermute(jnp.stack([c1[-1:], a0[-1:], a1[-1:]]), "space", down)
    bot_a = lax.ppermute(jnp.stack([c1[:1], a0[:1], a1[:1]]), "space", up)
    if merge:
        top_b = lax.ppermute(c2[None, -1:], "space", down)
        bot_b = lax.ppermute(c2[None, :1], "space", up)
        return pair_conv((c2, c1, a0, a1, top_a, bot_a, top_b, bot_b), x0, x1, w_mat)
    outs1 = frame_conv(1, (c1, a0, a1, top_a, bot_a), x1, w_mat, with_act)
    top_b = lax.ppermute(c2[None, -1:], "space", down)
    bot_b = lax.ppermute(c2[None, :1], "space", up)
    outs0 = frame_conv(0, (c2, c1, a0, top_a, bot_a, top_b, bot_b), x0, w_mat, with_act)
    return outs0, outs1


def both_taps(weights):
    local = tap_matrix(weights[0])
    half = local.shape[0] // 2
    section = lax.axis_index("section")
    core = lax.axis_index("space") % 2
    n_space = lax.axis_size("space")
    mine = lax.dynamic_slice_in_dim(local, core * half, half, axis=0)
    got = lax.ppermute(mine, "section", [(0, 1), (1, 0)])
    other = lax.ppermute(got, "space", [(i, i ^ 1) for i in range(n_space)])
    return (True, local, got, other), (False, local, got, other)


def body(video, weights):
    first, second = both_taps(weights)
    clip = video[0]
    assert clip.shape[0] == 2
    x0, x1 = clip[0], clip[1]
    a1 = silu(x1)
    a0 = silu(x0)
    (h0, s0), (h1, s1) = conv_block((x0, x1), (a0, a1), first, True, False)
    whole = conv_block((h0, h1), (s0, s1), second, False, True)
    return whole[None]


def solution(mesh):
    return jax.shard_map(
        body,
        mesh=mesh,
        in_specs=(P("section", "tm", "space", None, None), P("section", None, None, None)),
        out_specs=P("section", "tm", "space", None, None),
        check_vma=False,
    )
```

```python
import functools

import jax
import jax.numpy as jnp
from jax import lax
from jax.experimental import pallas as pl
from jax.experimental.pallas import tpu as pltpu
from jax.sharding import PartitionSpec as P


def shift_tm(x):
    n = lax.axis_size("tm")
    return lax.ppermute(x, "tm", [(i, i + 1) for i in range(n - 1)])


def silu(x):
    return jax.nn.silu(x.astype(jnp.float32)).astype(jnp.bfloat16)


def conv_rows(sources, base_ref, w_ref, store):
    rows, width, chans = base_ref.shape

    def slab(a, j):
        ref, top, bottom, halo = sources[a]
        if j == 0:
            return top[halo, 0]
        if j == rows + 1:
            return bottom[halo, 0]
        return ref[j - 1]

    column = lax.broadcasted_iota(jnp.int32, (width, chans), 0)
    for h in range(rows):
        lhs = jnp.concatenate([slab(a, h + r) for a in range(3) for r in range(3)], axis=-1)
        z = jnp.dot(lhs, w_ref[...], preferred_element_type=jnp.float32)
        left = pltpu.roll(z[:, :chans], 1, 0)
        right = pltpu.roll(z[:, 2 * chans :], width - 1, 0)
        left = jnp.where(column == 0, 0.0, left)
        right = jnp.where(column == width - 1, 0.0, right)
        total = z[:, chans : 2 * chans] + left + right
        store(h, base_ref[h].astype(jnp.float32) + total)


def frame_sources(t, c2_ref, c1_ref, a0_ref, a1_ref, top_a, bot_a, top_b, bot_b):
    if t == 1:
        return [(c1_ref, top_a, bot_a, 0), (a0_ref, top_a, bot_a, 1), (a1_ref, top_a, bot_a, 2)]
    return [(c2_ref, top_b, bot_b, 0), (c1_ref, top_a, bot_a, 0), (a0_ref, top_a, bot_a, 1)]


def assemble(first, local_ref, got_ref, other_ref, buf):
    section = lax.axis_index("section")
    core = lax.axis_index("space") % 2
    half = got_ref.shape[0]
    use_local = section == 0 if first else section != 0

    @pl.when(use_local)
    def _():
        buf[...] = local_ref[...]

    @pl.when(jnp.logical_and(jnp.logical_not(use_local), core == 0))
    def _():
        buf[:half] = got_ref[...]
        buf[half:] = other_ref[...]

    @pl.when(jnp.logical_and(jnp.logical_not(use_local), core != 0))
    def _():
        buf[:half] = other_ref[...]
        buf[half:] = got_ref[...]

    return buf


def frame_kernel(t, with_act, first, indexed, *refs):
    buf = refs[-1]
    refs = refs[:-1]
    if t == 1:
        c1_ref, a0_ref, a1_ref, top_a, bot_a, base_ref = refs[:6]
        w_ref = assemble(first, *refs[6:9], buf)
        sources = frame_sources(1, None, c1_ref, a0_ref, a1_ref, top_a, bot_a, None, None)
    else:
        c2_ref, c1_ref, a0_ref, top_a, bot_a, top_b, bot_b, base_ref = refs[:8]
        w_ref = assemble(first, *refs[8:11], buf)
        sources = frame_sources(0, c2_ref, c1_ref, a0_ref, None, top_a, bot_a, top_b, bot_b)
    outs = refs[len(refs) - (2 if with_act else 1) :]
    if indexed:
        base_ref = base_ref.at[t]

    def store(h, value):
        out = value.astype(outs[0].dtype)
        outs[0][h] = out
        if with_act:
            wide = out.astype(jnp.float32)
            outs[1][h] = (wide / (1.0 + jnp.exp(-wide))).astype(outs[1].dtype)

    conv_rows(sources, base_ref, w_ref, store)


def pair_kernel(first, c2_ref, c1_ref, a0_ref, a1_ref, top_a, bot_a, top_b, bot_b, x0_ref, x1_ref, local_ref, got_ref, other_ref, out_ref, buf):
    w_ref = assemble(first, local_ref, got_ref, other_ref, buf)
    for t, base_ref in ((1, x1_ref), (0, x0_ref)):
        sources = frame_sources(t, c2_ref, c1_ref, a0_ref, a1_ref, top_a, bot_a, top_b, bot_b)

        def store(h, value, t=t):
            out_ref[t, h] = value.astype(out_ref.dtype)

        conv_rows(sources, base_ref, w_ref, store)


def tap_matrix(taps):
    nine, three_c, chans = taps.shape
    return (
        taps.reshape(nine, 3, chans, chans)
        .transpose(0, 2, 1, 3)
        .reshape(nine * chans, 3 * chans)
    )


def frame_conv(t, operands, base, w_parts, with_act, indexed=False):
    rows, width, chans = base.shape[-3:]
    first, local, got, other = w_parts
    flops = 2 * rows * width * local.shape[0] * local.shape[1]
    nbytes = sum(x.size * x.dtype.itemsize for x in operands) + 3 * base.size * 2 + local.size * 4
    shape = jax.ShapeDtypeStruct(base.shape[-3:], base.dtype)
    return pl.pallas_call(
        functools.partial(frame_kernel, t, with_act, first, indexed),
        out_shape=(shape, shape) if with_act else (shape,),
        scratch_shapes=[pltpu.VMEM(local.shape, local.dtype)],
        cost_estimate=pl.CostEstimate(flops=flops, bytes_accessed=nbytes, transcendentals=0),
    )(*operands, base, local, got, other)


def pair_conv(operands, x0, x1, w_parts):
    rows, width, chans = x0.shape
    first, local, got, other = w_parts
    flops = 4 * rows * width * local.shape[0] * local.shape[1]
    nbytes = sum(x.size * x.dtype.itemsize for x in operands) + 4 * x0.size * 2 + local.size * 4
    return pl.pallas_call(
        functools.partial(pair_kernel, first),
        out_shape=jax.ShapeDtypeStruct((2,) + x0.shape, x0.dtype),
        scratch_shapes=[pltpu.VMEM(local.shape, local.dtype)],
        cost_estimate=pl.CostEstimate(flops=flops, bytes_accessed=nbytes, transcendentals=0),
    )(*operands, x0, x1, local, got, other)


def conv_block(frames_in, acts, w_mat, with_act, merge, whole=None):
    x0, x1 = frames_in
    a0, a1 = acts
    n = lax.axis_size("space")
    down = [(i, i + 1) for i in range(n - 1)]
    up = [(i + 1, i) for i in range(n - 1)]
    c1 = shift_tm(a1)
    a0, c1 = lax.optimization_barrier((a0, c1))
    c2 = shift_tm(a0)
    top_a = lax.ppermute(jnp.stack([c1[-1:], a0[-1:], a1[-1:]]), "space", down)
    bot_a = lax.ppermute(jnp.stack([c1[:1], a0[:1], a1[:1]]), "space", up)
    if merge:
        top_b = lax.ppermute(c2[None, -1:], "space", down)
        bot_b = lax.ppermute(c2[None, :1], "space", up)
        return pair_conv((c2, c1, a0, a1, top_a, bot_a, top_b, bot_b), x0, x1, w_mat)
    outs1 = frame_conv(1, (c1, a0, a1, top_a, bot_a), whole, w_mat, with_act, True)
    top_b = lax.ppermute(c2[None, -1:], "space", down)
    bot_b = lax.ppermute(c2[None, :1], "space", up)
    outs0 = frame_conv(0, (c2, c1, a0, top_a, bot_a, top_b, bot_b), whole, w_mat, with_act, True)
    return outs0, outs1


def both_taps(weights):
    local = tap_matrix(weights[0])
    half = local.shape[0] // 2
    section = lax.axis_index("section")
    core = lax.axis_index("space") % 2
    n_space = lax.axis_size("space")
    mine = lax.dynamic_slice_in_dim(local, core * half, half, axis=0)
    got = lax.ppermute(mine, "section", [(0, 1), (1, 0)])
    other = lax.ppermute(got, "space", [(i, i ^ 1) for i in range(n_space)])
    return (True, local, got, other), (False, local, got, other)


def body(video, weights):
    first, second = both_taps(weights)
    clip = video[0]
    assert clip.shape[0] == 2
    x0, x1 = clip[0], clip[1]
    a1 = silu(x1)
    a0 = silu(x0)
    (h0, s0), (h1, s1) = conv_block((x0, x1), (a0, a1), first, True, False, clip)
    whole = conv_block((h0, h1), (s0, s1), second, False, True)
    return whole[None]


def solution(mesh):
    return jax.shard_map(
        body,
        mesh=mesh,
        in_specs=(P("section", "tm", "space", None, None), P("section", None, None, None)),
        out_specs=P("section", "tm", "space", None, None),
        check_vma=False,
    )
```

```python
import functools

import jax
import jax.numpy as jnp
from jax import lax
from jax.experimental import pallas as pl
from jax.experimental.pallas import tpu as pltpu
from jax.sharding import PartitionSpec as P


def shift_tm(x):
    n = lax.axis_size("tm")
    return lax.ppermute(x, "tm", [(i, i + 1) for i in range(n - 1)])


def silu(x):
    return jax.nn.silu(x.astype(jnp.float32)).astype(jnp.bfloat16)


def conv_rows(sources, base_ref, w_ref, store):
    rows, width, chans = base_ref.shape

    def slab(a, j):
        ref, top, bottom, halo = sources[a]
        if j == 0:
            return top[halo, 0]
        if j == rows + 1:
            return bottom[halo, 0]
        return ref[j - 1]

    column = lax.broadcasted_iota(jnp.int32, (width, chans), 0)
    for h in range(rows):
        lhs = jnp.concatenate([slab(a, h + r) for a in range(3) for r in range(3)], axis=-1)
        z = jnp.dot(lhs, w_ref[...], preferred_element_type=jnp.float32)
        left = pltpu.roll(z[:, :chans], 1, 0)
        right = pltpu.roll(z[:, 2 * chans :], width - 1, 0)
        left = jnp.where(column == 0, 0.0, left)
        right = jnp.where(column == width - 1, 0.0, right)
        total = z[:, chans : 2 * chans] + left + right
        store(h, base_ref[h].astype(jnp.float32) + total)


def frame_sources(t, c2_ref, c1_ref, a0_ref, a1_ref, top_a, bot_a, top_b, bot_b):
    if t == 1:
        return [(c1_ref, top_a, bot_a, 0), (a0_ref, top_a, bot_a, 1), (a1_ref, top_a, bot_a, 2)]
    return [(c2_ref, top_b, bot_b, 0), (c1_ref, top_a, bot_a, 0), (a0_ref, top_a, bot_a, 1)]


def assemble(first, local_ref, got_ref, other_ref, buf):
    section = lax.axis_index("section")
    core = lax.axis_index("space") % 2
    nine, three_c, chans = local_ref.shape
    half = got_ref.shape[1]
    use_local = section == 0 if first else section != 0

    def fill_full(src):
        for k in range(nine):
            for s in range(3):
                buf[k * chans : (k + 1) * chans, s * chans : (s + 1) * chans] = src[k, s * chans : (s + 1) * chans, :]

    def fill_halves(lo, hi):
        for k in range(nine):
            for s in range(3):
                for i in range(0, chans, 64):
                    row = s * chans + i
                    part, at = (lo, row) if row < half else (hi, row - half)
                    buf[k * chans + i : k * chans + i + 64, s * chans : (s + 1) * chans] = part[k, at : at + 64, :]

    @pl.when(use_local)
    def _():
        fill_full(local_ref)

    @pl.when(jnp.logical_and(jnp.logical_not(use_local), core == 0))
    def _():
        fill_halves(got_ref, other_ref)

    @pl.when(jnp.logical_and(jnp.logical_not(use_local), core != 0))
    def _():
        fill_halves(other_ref, got_ref)

    return buf


def frame_kernel(t, with_act, first, *refs):
    buf = refs[-1]
    refs = refs[:-1]
    if t == 1:
        c1_ref, a0_ref, a1_ref, top_a, bot_a, base_ref = refs[:6]
        w_ref = assemble(first, *refs[6:9], buf)
        sources = frame_sources(1, None, c1_ref, a0_ref, a1_ref, top_a, bot_a, None, None)
    else:
        c2_ref, c1_ref, a0_ref, top_a, bot_a, top_b, bot_b, base_ref = refs[:8]
        w_ref = assemble(first, *refs[8:11], buf)
        sources = frame_sources(0, c2_ref, c1_ref, a0_ref, None, top_a, bot_a, top_b, bot_b)
    outs = refs[len(refs) - (2 if with_act else 1) :]

    def store(h, value):
        out = value.astype(outs[0].dtype)
        outs[0][h] = out
        if with_act:
            wide = out.astype(jnp.float32)
            outs[1][h] = (wide / (1.0 + jnp.exp(-wide))).astype(outs[1].dtype)

    conv_rows(sources, base_ref, w_ref, store)


def pair_kernel(first, c2_ref, c1_ref, a0_ref, a1_ref, top_a, bot_a, top_b, bot_b, x0_ref, x1_ref, local_ref, got_ref, other_ref, out_ref, buf):
    w_ref = assemble(first, local_ref, got_ref, other_ref, buf)
    for t, base_ref in ((1, x1_ref), (0, x0_ref)):
        sources = frame_sources(t, c2_ref, c1_ref, a0_ref, a1_ref, top_a, bot_a, top_b, bot_b)

        def store(h, value, t=t):
            out_ref[t, h] = value.astype(out_ref.dtype)

        conv_rows(sources, base_ref, w_ref, store)


def tap_matrix(taps):
    nine, three_c, chans = taps.shape
    return (
        taps.reshape(nine, 3, chans, chans)
        .transpose(0, 2, 1, 3)
        .reshape(nine * chans, 3 * chans)
    )


def frame_conv(t, operands, base, w_parts, with_act):
    rows, width, chans = base.shape
    first, local, got, other = w_parts
    w_shape = (local.shape[0] * local.shape[2], local.shape[1])
    flops = 2 * rows * width * w_shape[0] * w_shape[1]
    nbytes = sum(x.size * x.dtype.itemsize for x in operands) + 3 * base.size * 2 + local.size * 4
    shape = jax.ShapeDtypeStruct(base.shape, base.dtype)
    return pl.pallas_call(
        functools.partial(frame_kernel, t, with_act, first),
        out_shape=(shape, shape) if with_act else (shape,),
        scratch_shapes=[pltpu.VMEM(w_shape, local.dtype)],
        cost_estimate=pl.CostEstimate(flops=flops, bytes_accessed=nbytes, transcendentals=0),
    )(*operands, base, local, got, other)


def pair_conv(operands, x0, x1, w_parts):
    rows, width, chans = x0.shape
    first, local, got, other = w_parts
    w_shape = (local.shape[0] * local.shape[2], local.shape[1])
    flops = 4 * rows * width * w_shape[0] * w_shape[1]
    nbytes = sum(x.size * x.dtype.itemsize for x in operands) + 4 * x0.size * 2 + local.size * 4
    return pl.pallas_call(
        functools.partial(pair_kernel, first),
        out_shape=jax.ShapeDtypeStruct((2,) + x0.shape, x0.dtype),
        scratch_shapes=[pltpu.VMEM(w_shape, local.dtype)],
        cost_estimate=pl.CostEstimate(flops=flops, bytes_accessed=nbytes, transcendentals=0),
    )(*operands, x0, x1, local, got, other)


def conv_block(frames_in, acts, w_mat, with_act, merge):
    x0, x1 = frames_in
    a0, a1 = acts
    n = lax.axis_size("space")
    down = [(i, i + 1) for i in range(n - 1)]
    up = [(i + 1, i) for i in range(n - 1)]
    c1 = shift_tm(a1)
    a0, c1 = lax.optimization_barrier((a0, c1))
    c2 = shift_tm(a0)
    top_a = lax.ppermute(jnp.stack([c1[-1:], a0[-1:], a1[-1:]]), "space", down)
    bot_a = lax.ppermute(jnp.stack([c1[:1], a0[:1], a1[:1]]), "space", up)
    if merge:
        top_b = lax.ppermute(c2[None, -1:], "space", down)
        bot_b = lax.ppermute(c2[None, :1], "space", up)
        return pair_conv((c2, c1, a0, a1, top_a, bot_a, top_b, bot_b), x0, x1, w_mat)
    outs1 = frame_conv(1, (c1, a0, a1, top_a, bot_a), x1, w_mat, with_act)
    top_b = lax.ppermute(c2[None, -1:], "space", down)
    bot_b = lax.ppermute(c2[None, :1], "space", up)
    outs0 = frame_conv(0, (c2, c1, a0, top_a, bot_a, top_b, bot_b), x0, w_mat, with_act)
    return outs0, outs1


def both_taps(weights):
    local = weights[0]
    half = local.shape[1] // 2
    section = lax.axis_index("section")
    core = lax.axis_index("space") % 2
    n_space = lax.axis_size("space")
    mine = lax.dynamic_slice_in_dim(local, core * half, half, axis=1)
    got = lax.ppermute(mine, "section", [(0, 1), (1, 0)])
    other = lax.ppermute(got, "space", [(i, i ^ 1) for i in range(n_space)])
    return (True, local, got, other), (False, local, got, other)


def body(video, weights):
    first, second = both_taps(weights)
    clip = video[0]
    assert clip.shape[0] == 2
    x0, x1 = clip[0], clip[1]
    a1 = silu(x1)
    a0 = silu(x0)
    (h0, s0), (h1, s1) = conv_block((x0, x1), (a0, a1), first, True, False)
    whole = conv_block((h0, h1), (s0, s1), second, False, True)
    return whole[None]


def solution(mesh):
    return jax.shard_map(
        body,
        mesh=mesh,
        in_specs=(P("section", "tm", "space", None, None), P("section", None, None, None)),
        out_specs=P("section", "tm", "space", None, None),
        check_vma=False,
    )
```

```python
import functools

import jax
import jax.numpy as jnp
from jax import lax
from jax.experimental import pallas as pl
from jax.experimental.pallas import tpu as pltpu
from jax.sharding import PartitionSpec as P


def shift_tm(x):
    n = lax.axis_size("tm")
    return lax.ppermute(x, "tm", [(i, i + 1) for i in range(n - 1)])


def silu(x):
    return jax.nn.silu(x.astype(jnp.float32)).astype(jnp.bfloat16)


def conv_rows(sources, base_ref, w_ref, store):
    rows, width, chans = base_ref.shape

    def slab(a, j):
        ref, top, bottom, halo = sources[a]
        if j == 0:
            return top[halo, 0]
        if j == rows + 1:
            return bottom[halo, 0]
        return ref[j - 1]

    column = lax.broadcasted_iota(jnp.int32, (width, chans), 0)
    for h in range(rows):
        lhs = jnp.concatenate([slab(a, h + r) for a in range(3) for r in range(3)], axis=-1)
        z = jnp.dot(lhs, w_ref[...], preferred_element_type=jnp.float32)
        left = pltpu.roll(z[:, :chans], 1, 0)
        right = pltpu.roll(z[:, 2 * chans :], width - 1, 0)
        left = jnp.where(column == 0, 0.0, left)
        right = jnp.where(column == width - 1, 0.0, right)
        total = z[:, chans : 2 * chans] + left + right
        store(h, base_ref[h].astype(jnp.float32) + total)


def frame_sources(t, c2_ref, c1_ref, a0_ref, a1_ref, top_a, bot_a, top_b, bot_b):
    if t == 1:
        return [(c1_ref, top_a, bot_a, 0), (a0_ref, top_a, bot_a, 1), (a1_ref, top_a, bot_a, 2)]
    return [(c2_ref, top_b, bot_b, 0), (c1_ref, top_a, bot_a, 0), (a0_ref, top_a, bot_a, 1)]


def assemble(first, local_ref, got_ref, other_ref, buf):
    section = lax.axis_index("section")
    core = lax.axis_index("space") % 2
    half = got_ref.shape[0]
    use_local = section == 0 if first else section != 0

    @pl.when(use_local)
    def _():
        buf[...] = local_ref[...]

    @pl.when(jnp.logical_and(jnp.logical_not(use_local), core == 0))
    def _():
        buf[:half] = got_ref[...]
        buf[half:] = other_ref[...]

    @pl.when(jnp.logical_and(jnp.logical_not(use_local), core != 0))
    def _():
        buf[:half] = other_ref[...]
        buf[half:] = got_ref[...]

    return buf


def frame_kernel(t, with_act, first, *refs):
    buf = refs[-1]
    refs = refs[:-1]
    if t == 1:
        c1_ref, a0_ref, a1_ref, top_a, bot_a, base_ref = refs[:6]
        w_ref = assemble(first, *refs[6:9], buf)
        sources = frame_sources(1, None, c1_ref, a0_ref, a1_ref, top_a, bot_a, None, None)
    else:
        c2_ref, c1_ref, a0_ref, top_a, bot_a, top_b, bot_b, base_ref = refs[:8]
        w_ref = assemble(first, *refs[8:11], buf)
        sources = frame_sources(0, c2_ref, c1_ref, a0_ref, None, top_a, bot_a, top_b, bot_b)
    outs = refs[len(refs) - (2 if with_act else 1) :]

    def store(h, value):
        out = value.astype(outs[0].dtype)
        outs[0][h] = out
        if with_act:
            wide = out.astype(jnp.float32)
            outs[1][h] = (wide / (1.0 + jnp.exp(-wide))).astype(outs[1].dtype)

    conv_rows(sources, base_ref, w_ref, store)


def pair_kernel(first, c2_ref, c1_ref, a0_ref, a1_ref, top_a, bot_a, top_b, bot_b, x0_ref, x1_ref, local_ref, got_ref, other_ref, out_ref, buf):
    w_ref = assemble(first, local_ref, got_ref, other_ref, buf)
    for t, base_ref in ((1, x1_ref), (0, x0_ref)):
        sources = frame_sources(t, c2_ref, c1_ref, a0_ref, a1_ref, top_a, bot_a, top_b, bot_b)

        def store(h, value, t=t):
            out_ref[t, h] = value.astype(out_ref.dtype)

        conv_rows(sources, base_ref, w_ref, store)


def tap_matrix(taps):
    nine, three_c, chans = taps.shape
    return (
        taps.reshape(nine, 3, chans, chans)
        .transpose(0, 2, 1, 3)
        .reshape(nine * chans, 3 * chans)
    )


def frame_conv(t, operands, base, w_parts, with_act):
    rows, width, chans = base.shape
    first, local, got, other = w_parts
    flops = 2 * rows * width * local.shape[0] * local.shape[1]
    nbytes = sum(x.size * x.dtype.itemsize for x in operands) + 3 * base.size * 2 + local.size * 4
    shape = jax.ShapeDtypeStruct(base.shape, base.dtype)
    return pl.pallas_call(
        functools.partial(frame_kernel, t, with_act, first),
        out_shape=(shape, shape) if with_act else (shape,),
        scratch_shapes=[pltpu.VMEM(local.shape, local.dtype)],
        cost_estimate=pl.CostEstimate(flops=flops, bytes_accessed=nbytes, transcendentals=0),
    )(*operands, base, local, got, other)


def pair_conv(operands, x0, x1, w_parts):
    rows, width, chans = x0.shape
    first, local, got, other = w_parts
    flops = 4 * rows * width * local.shape[0] * local.shape[1]
    nbytes = sum(x.size * x.dtype.itemsize for x in operands) + 4 * x0.size * 2 + local.size * 4
    return pl.pallas_call(
        functools.partial(pair_kernel, first),
        out_shape=jax.ShapeDtypeStruct((2,) + x0.shape, x0.dtype),
        scratch_shapes=[pltpu.VMEM(local.shape, local.dtype)],
        cost_estimate=pl.CostEstimate(flops=flops, bytes_accessed=nbytes, transcendentals=0),
    )(*operands, x0, x1, local, got, other)


def conv_block(frames_in, acts, w_mat, with_act, merge):
    x0, x1 = frames_in
    a0, a1 = acts
    n = lax.axis_size("space")
    down = [(i, i + 1) for i in range(n - 1)]
    up = [(i + 1, i) for i in range(n - 1)]
    c1 = shift_tm(a1)
    a0, c1 = lax.optimization_barrier((a0, c1))
    c2 = shift_tm(a0)
    top_a = lax.ppermute(jnp.stack([c1[-1:], a0[-1:], a1[-1:]]), "space", down)
    bot_a = lax.ppermute(jnp.stack([c1[:1], a0[:1], a1[:1]]), "space", up)
    if merge:
        top_b = lax.ppermute(c2[None, -1:], "space", down)
        bot_b = lax.ppermute(c2[None, :1], "space", up)
        return pair_conv((c2, c1, a0, a1, top_a, bot_a, top_b, bot_b), x0, x1, w_mat)
    outs1 = frame_conv(1, (c1, a0, a1, top_a, bot_a), x1, w_mat, with_act)
    top_b = lax.ppermute(c2[None, -1:], "space", down)
    bot_b = lax.ppermute(c2[None, :1], "space", up)
    outs0 = frame_conv(0, (c2, c1, a0, top_a, bot_a, top_b, bot_b), x0, w_mat, with_act)
    return outs0, outs1


def both_taps(weights):
    local = tap_matrix(weights[0])
    half = local.shape[0] // 2
    section = lax.axis_index("section")
    core = lax.axis_index("space") % 2
    n_space = lax.axis_size("space")
    mine = lax.dynamic_slice_in_dim(local, core * half, half, axis=0)
    got = lax.ppermute(mine, "section", [(0, 1), (1, 0)])
    other = lax.ppermute(got, "space", [(i, i ^ 1) for i in range(n_space)])
    return (True, local, got, other), (False, local, got, other)


def body(video, weights):
    first, second = both_taps(weights)
    clip = video[0]
    assert clip.shape[0] == 2
    x0, x1 = clip[0], clip[1]
    a1 = silu(x1)
    x0, a1 = lax.optimization_barrier((x0, a1))
    a0 = silu(x0)
    (h0, s0), (h1, s1) = conv_block((x0, x1), (a0, a1), first, True, False)
    whole = conv_block((h0, h1), (s0, s1), second, False, True)
    return whole[None]


def solution(mesh):
    return jax.shard_map(
        body,
        mesh=mesh,
        in_specs=(P("section", "tm", "space", None, None), P("section", None, None, None)),
        out_specs=P("section", "tm", "space", None, None),
        check_vma=False,
    )
```
